32 devices in a mesh: obs: 16 (over z, x, core), freq: 2 (over y).
Axes of the slice: x: 2, y: 2, z: 4, core: 2. Of those that a mesh axis runs over, the one named last changes fastest.
Arguments:
- cell_spectra: bfloat16 [8192, 512], P('obs', 'freq'), may hold values from -6 to 6
- cell_weight: float32 [8192], P('obs'), may hold values from 0.25 to 1
- cell_owner: int32 [8192, 1], P('obs'), may hold values from 0 to 15; in each aligned block of 512 rows (0 to 511, 512 to 1023, ...) at most 80 rows name the same one
- cell_local: int32 [8192], P('obs'), may hold values from 0 to 31
- panel_position: float32 [3, 512], replicated, may hold values from -8 to 8
- observer_position: float32 [3, 1024], P(None, 'obs'), may hold values from -40 to 40, as said below
Outputs:
- pressure: float32 [64, 2, 1024], P('freq', None, 'obs')
- level: float32 [1024], P('obs')
The draws below stay inside these ranges and needn't reach their ends.
Inputs may be any that keep to these rules, and one draw needn't show every extreme that they name: `cell_owner`: among the 512 cells of one partition at most 80 name one panel group, and in every draw some partition sends exactly 80 cells to one group. `observer_position`: every observer lies between 20 and 40 from the anchor (0, 0, 0).
All inputs are finite; a program needn't handle non-finite values.
Results may differ from the reference program's by a relative error of at most 0.0029.
Values may be sent and summed in bfloat16 or wider, within the bound.
No kernel may reach another device: no remote copies, remote signals or barrier semaphores. Data moves between devices by JAX's collectives and lax.ppermute only.
A program may use at most 64 MiB of HBM per device.

```python
import math
import jax
import jax.numpy as jnp
import numpy as np
from jax import lax

FREQS = 64
CELLS_DEV = 512
PANELS_DEV = 32
GROUPS = 16
CAP = 80
CELLS = 8192
PANELS = 512
OBS = 1024


def draw_observer_position(key, part):
    first_key, second_key, third_key = jax.random.split(key, 3)
    polar = jax.random.uniform(first_key, (OBS,), jnp.float32, 0.35, 2.8)
    azimuth = jax.random.uniform(second_key, (OBS,), jnp.float32, -3.14159, 3.14159)
    radius = jax.random.uniform(third_key, (OBS,), jnp.float32, 20.0, 40.0)
    along = radius * jnp.cos(polar)
    across = radius * jnp.sin(polar)
    return jnp.stack([along, across * jnp.cos(azimuth), across * jnp.sin(azimuth)]).astype(jnp.float32)


def plant(values, stream_key, smallest, largest):
    shape = values.shape
    index_at = [jax.random.randint(jax.random.fold_in(stream_key, axis), (), 0, shape[axis]) for axis in range(len(shape))]
    values = values.at[tuple(index_at)].set(smallest)
    longest = shape.index(max(shape))
    index_at[longest] = (index_at[longest] + 1) % shape[longest]
    return values.at[tuple(index_at)].set(largest)


def block_levels(own_key, shape, cuts, smallest, top_value):
    def one(position, blocks):
        heights = jax.random.uniform(jax.random.fold_in(jax.random.fold_in(own_key, 6), position), (blocks,), jnp.float32, smallest / len(cuts), top_value / len(cuts))
        return jnp.repeat(jnp.exp(heights), shape[position] // blocks).reshape((-1,) + (1,) * (len(shape) - position - 1))

    gain = one(*cuts[0])
    for cut in cuts[1:]:
        gain = gain * one(*cut)
    return gain


def assign_block(stream_key, own, number, rows, count, top, most, lean):
    sequence = jax.random.permutation(stream_key, count)
    heavy_load, usual = portions_of(count, rows * top, most, lean, True), portions_of(count, rows * top, most, lean, False)
    places = jnp.arange(count)

    def named(tallies, rotation):
        used = int((tallies > 0).sum())
        fixed = max(1, used // 4)
        moved = fixed + (places - fixed + rotation * (used - fixed)) % max(1, count - fixed)
        return jnp.zeros((count,), jnp.int32).at[sequence[jnp.where(places < fixed, places, moved)]].set(jnp.asarray(tallies, jnp.int32))

    tallies = jnp.where(number % 4 == 0, named(heavy_load, number // 4), named(usual, number - number // 4 - 1))
    mixed = jax.random.permutation(jax.random.fold_in(own, 3), count)
    source_of, taker = mixed[0:count // 2 * 2:2], mixed[1:count // 2 * 2:2]
    margin = jnp.minimum(tallies[source_of] - 1, most - tallies[taker]) // 2
    margin = jnp.where((source_of == sequence[0]) | (taker == sequence[0]) | (tallies[taker] == 0), 0, jnp.maximum(margin, 0))
    moved = jax.random.randint(jax.random.fold_in(own, 4), (count // 2,), 0, 1 << 20) % (margin + 1)
    tallies = tallies.at[source_of].add(-moved).at[taker].add(moved)
    members = jnp.searchsorted(jnp.cumsum(tallies), jnp.arange(rows * top), side="right").astype(jnp.int32)
    grid = members.reshape(top, rows).T
    grid = grid[jax.random.permutation(jax.random.fold_in(own, 1), rows)]
    rotation = jax.random.randint(jax.random.fold_in(own, 2), (rows, 1), 0, top)
    return jnp.take_along_axis(grid, (jnp.arange(top)[None, :] + rotation) % top, axis=1)


def portions_of(count, total, reach, lean, full):
    weights = [(1 << 20) // math.isqrt(grade ** lean) + 1 for grade in range(1, count + 1)]
    largest = reach if full else min(reach, max(-(-total // count), total * weights[0] // sum(weights)))
    least = 1 if total - largest >= count - 1 else 0
    counts, spare = [largest] + [least] * (count - 1), total - largest - least * (count - 1)
    while spare > 0:
        candidates = [i for i in range(1, count) if counts[i] < largest] or [i for i in range(1, count) if counts[i] < reach]
        mass, left = sum([weights[i] for i in candidates]), spare
        for i in candidates:
            extra = min(reach - counts[i], max(1, left * weights[i] // mass), spare)
            counts[i] = counts[i] + extra
            spare = spare - extra
    return np.array(counts)


def scatter_about(key, shape, scale, limit, cuts=(), kind=jnp.bfloat16):
    entries = jax.random.normal(key, shape, jnp.float32) * scale
    if len(cuts) > 0:
        entries = block_levels(key, shape, cuts, -0.22, 0.18) * entries
    return jnp.clip(entries, min=-limit, max=limit).astype(kind)


def setup_inputs(seed: int = 0) -> dict:
    arg_keys = jax.random.split(jax.random.key(seed), 7)
    cell_spectra = scatter_about(arg_keys[0], (CELLS, FREQS * 8), 1.0, 6.0, ((0, 16), (1, 2)))
    cell_weight = jnp.clip(jnp.exp(math.log(1.0) - 1.3862944 * jax.random.uniform(arg_keys[1], (CELLS,), jnp.float32) ** block_levels(arg_keys[1], (CELLS,), ((0, 16),), -0.2, 0.2)), 0.25, 1.0)
    cell_owner_keys = jax.random.split(jax.random.fold_in(arg_keys[2], 1), CELLS // CELLS_DEV)
    cell_owner_turns = jax.random.permutation(jax.random.fold_in(arg_keys[2], 3), CELLS // CELLS_DEV)
    cell_owner = jax.vmap(lambda own, number: assign_block(jax.random.fold_in(arg_keys[2], 2), own, number, CELLS_DEV, GROUPS, 1, CAP, 1))(cell_owner_keys, cell_owner_turns).reshape((CELLS, 1))
    cell_local = plant(jax.random.randint(arg_keys[3], (CELLS,), 0, PANELS_DEV), jax.random.fold_in(arg_keys[3], 1), 0, PANELS_DEV - 1).astype(jnp.int32)
    panel_position = jnp.clip(jax.random.uniform(arg_keys[4], (3, PANELS), jnp.float32, -8.0, 8.0), -8.0, 8.0)
    observer_position = draw_observer_position(jax.random.fold_in(arg_keys[6], 71), 0)
    return dict(cell_spectra=cell_spectra, cell_weight=cell_weight, cell_owner=cell_owner, cell_local=cell_local, panel_position=panel_position, observer_position=observer_position)


wave_step = 0.1
reference_radius = 10.0

def kernel_block(source, panel_points, observer_points, wave_numbers):
    offsets = observer_points[:, None, :] - panel_points[:, :, None]
    distance = jnp.sqrt(offsets[0] * offsets[0] + offsets[1] * offsets[1] + offsets[2] * offsets[2])
    inverse = 1.0 / distance
    heading = offsets * inverse[None]
    channels = jnp.transpose(source, (2, 1, 0))
    dipole_real = heading[0][None] * channels[2][:, :, None] + heading[1][None] * channels[4][:, :, None] + heading[2][None] * channels[6][:, :, None]
    dipole_imag = heading[0][None] * channels[3][:, :, None] + heading[1][None] * channels[5][:, :, None] + heading[2][None] * channels[7][:, :, None]
    waves = wave_numbers[:, None, None]
    amp_real = channels[0][:, :, None] + dipole_real * inverse[None] - waves * dipole_imag
    amp_imag = channels[1][:, :, None] + dipole_imag * inverse[None] + waves * dipole_real
    phases = waves * distance[None]
    weight_real = jnp.cos(phases) * inverse[None]
    weight_imag = jnp.sin(phases) * inverse[None]
    real_part = lax.optimization_barrier(jnp.sum(weight_real * amp_real + weight_imag * amp_imag, axis=1))
    imag_part = lax.optimization_barrier(jnp.sum(weight_real * amp_imag - weight_imag * amp_real, axis=1))
    return jnp.stack([real_part, imag_part], axis=1)

def reference(cell_spectra, cell_weight, cell_owner, cell_local, panel_position, observer_position):
    weighted = cell_weight[:, None] * cell_spectra.astype(jnp.float32)
    contribution = lax.optimization_barrier(weighted.astype(jnp.bfloat16)).astype(jnp.float32)
    panel_index = (cell_owner[:, 0] * PANELS_DEV + cell_local).astype(jnp.int32)
    panel_source = jax.ops.segment_sum(contribution, panel_index, num_segments=PANELS)
    panel_source = panel_source.reshape(PANELS, FREQS, 8)
    wave_numbers = wave_step * (jnp.arange(FREQS).astype(jnp.float32) + 1.0)
    observer_block = math.gcd(OBS, 256)
    panel_block = math.gcd(PANELS, 256)
    observer_tiles = jnp.transpose(observer_position.reshape(3, OBS // observer_block, observer_block), (1, 0, 2))
    source_tiles = panel_source.reshape(PANELS // panel_block, panel_block, FREQS, 8)
    panel_tiles = jnp.transpose(panel_position.reshape(3, PANELS // panel_block, panel_block), (1, 0, 2))

    def one_tile(observer_points):

        def accumulate(running, item):
            source, panel_points = item
            return (running + kernel_block(source, panel_points, observer_points, wave_numbers), None)
        start_value = jnp.zeros((FREQS, 2, observer_block), jnp.float32)
        result, _ = lax.scan(accumulate, start_value, (source_tiles, panel_tiles))
        return result
    tiles = lax.map(one_tile, observer_tiles)
    pressure = jnp.transpose(tiles, (1, 2, 0, 3)).reshape(FREQS, 2, OBS) * (reference_radius / math.sqrt(PANELS))
    energy = lax.optimization_barrier(jnp.sum(pressure[:, 0] * pressure[:, 0] + pressure[:, 1] * pressure[:, 1], axis=0)) / FREQS
    level = jnp.log(energy + 1e-06)
    return (pressure, level)
```

```python
import math

import jax
import jax.numpy as jnp
from jax import lax
from jax.sharding import PartitionSpec as P

wave_step = 0.1
reference_radius = 10.0


def phase_powers(distance, wave_numbers):
    needed = wave_numbers.shape[0]
    cosine = jnp.cos(wave_numbers[0] * distance)[None]
    sine = jnp.sin(wave_numbers[0] * distance)[None]
    step_cos = jnp.cos(wave_step * distance)[None]
    step_sin = jnp.sin(wave_step * distance)[None]
    while cosine.shape[0] < needed:
        later_cos = cosine * step_cos - sine * step_sin
        later_sin = sine * step_cos + cosine * step_sin
        cosine = jnp.concatenate([cosine, later_cos], axis=0)
        sine = jnp.concatenate([sine, later_sin], axis=0)
        step_cos, step_sin = (step_cos * step_cos - step_sin * step_sin, 2.0 * step_cos * step_sin)
    return (cosine, sine)


def kernel_block(source, panel_points, observer_points, wave_numbers):
    offsets = observer_points[:, None, :] - panel_points[:, :, None]
    distance = jnp.sqrt(offsets[0] * offsets[0] + offsets[1] * offsets[1] + offsets[2] * offsets[2])
    inverse = 1.0 / distance
    heading = offsets * inverse[None]
    channels = jnp.transpose(source, (2, 1, 0))
    dipole_real = (
        heading[0][None] * channels[2][:, :, None]
        + heading[1][None] * channels[4][:, :, None]
        + heading[2][None] * channels[6][:, :, None]
    )
    dipole_imag = (
        heading[0][None] * channels[3][:, :, None]
        + heading[1][None] * channels[5][:, :, None]
        + heading[2][None] * channels[7][:, :, None]
    )
    waves = wave_numbers[:, None, None]
    amp_real = channels[0][:, :, None] + dipole_real * inverse[None] - waves * dipole_imag
    amp_imag = channels[1][:, :, None] + dipole_imag * inverse[None] + waves * dipole_real
    cosine, sine = phase_powers(distance, wave_numbers)
    weight_real = cosine * inverse[None]
    weight_imag = sine * inverse[None]
    real_part = jnp.sum(weight_real * amp_real + weight_imag * amp_imag, axis=1)
    imag_part = jnp.sum(weight_real * amp_imag - weight_imag * amp_real, axis=1)
    return jnp.stack([real_part, imag_part], axis=1)


def shards(cell_spectra, cell_weight, cell_owner, cell_local, panel_position, observer_position):
    cell_rows, columns = cell_spectra.shape
    freqs_dev = columns // 8
    groups = lax.axis_size("obs")
    capacity = 5 * cell_rows // (2 * groups)
    panel_total = panel_position.shape[1]
    panels_dev = panel_total // groups
    observers_dev = observer_position.shape[1]
    weighted = (cell_weight[:, None] * cell_spectra.astype(jnp.float32)).astype(jnp.bfloat16)
    panel_index = cell_owner[:, 0] * panels_dev + cell_local
    selector = (
        jnp.arange(panel_total, dtype=jnp.int32)[:, None] == panel_index[None, :]
    ).astype(jnp.bfloat16)
    local_source = jnp.dot(selector, weighted, preferred_element_type=jnp.float32)
    group_first = lax.axis_index("freq") * freqs_dev
    wave_numbers = wave_step * (
        (group_first + jnp.arange(freqs_dev, dtype=jnp.int32)).astype(jnp.float32) + 1.0
    )
    start_value = jnp.zeros((freqs_dev, 2, observers_dev), jnp.float32)
    portion = lax.psum(local_source, "obs")
    rows_count = portion.shape[0]
    tile_rows = math.gcd(rows_count, 256)

    def advance(turn, accum):
        source = lax.dynamic_slice_in_dim(portion, turn * tile_rows, tile_rows, 0).reshape(
            tile_rows, freqs_dev, 8
        )
        points = lax.dynamic_slice_in_dim(panel_position, turn * tile_rows, tile_rows, 1)
        return accum + kernel_block(source, points, observer_position, wave_numbers)

    summed = lax.fori_loop(0, rows_count // tile_rows, advance, start_value)
    pressure = summed * (reference_radius / math.sqrt(panel_total))
    energy = jnp.sum(pressure[:, 0] * pressure[:, 0] + pressure[:, 1] * pressure[:, 1], axis=0)
    band_total = lax.psum(energy, "freq")
    level = jnp.log(band_total / (freqs_dev * lax.axis_size("freq")) + 1e-06)
    return (pressure, level)


def solution(mesh):
    in_specs = (P("obs", "freq"), P("obs"), P("obs", None), P("obs"), P(), P(None, "obs"))
    out_specs = (P("freq", None, "obs"), P("obs"))
    return jax.shard_map(shards, mesh=mesh, in_specs=in_specs, out_specs=out_specs, check_vma=False)
```

```python
import math

import jax
import jax.numpy as jnp
from jax import lax
from jax.sharding import PartitionSpec as P

wave_step = 0.1
reference_radius = 10.0


def phase_powers(distance, wave_numbers):
    needed = wave_numbers.shape[0]
    cosine = jnp.cos(wave_numbers[0] * distance)[None]
    sine = jnp.sin(wave_numbers[0] * distance)[None]
    step_cos = jnp.cos(wave_step * distance)[None]
    step_sin = jnp.sin(wave_step * distance)[None]
    while cosine.shape[0] < needed:
        later_cos = cosine * step_cos - sine * step_sin
        later_sin = sine * step_cos + cosine * step_sin
        cosine = jnp.concatenate([cosine, later_cos], axis=0)
        sine = jnp.concatenate([sine, later_sin], axis=0)
        step_cos, step_sin = (step_cos * step_cos - step_sin * step_sin, 2.0 * step_cos * step_sin)
    return (cosine, sine)


def kernel_block(source, panel_points, observer_points, wave_numbers):
    offsets = observer_points[:, None, :] - panel_points[:, :, None]
    distance = jnp.sqrt(offsets[0] * offsets[0] + offsets[1] * offsets[1] + offsets[2] * offsets[2])
    inverse = 1.0 / distance
    heading = offsets * inverse[None]
    channels = jnp.transpose(source, (2, 1, 0))
    dipole_real = (
        heading[0][None] * channels[2][:, :, None]
        + heading[1][None] * channels[4][:, :, None]
        + heading[2][None] * channels[6][:, :, None]
    )
    dipole_imag = (
        heading[0][None] * channels[3][:, :, None]
        + heading[1][None] * channels[5][:, :, None]
        + heading[2][None] * channels[7][:, :, None]
    )
    waves = wave_numbers[:, None, None]
    amp_real = channels[0][:, :, None] + dipole_real * inverse[None] - waves * dipole_imag
    amp_imag = channels[1][:, :, None] + dipole_imag * inverse[None] + waves * dipole_real
    cosine, sine = phase_powers(distance, wave_numbers)
    weight_real = cosine * inverse[None]
    weight_imag = sine * inverse[None]
    real_part = jnp.sum(weight_real * amp_real + weight_imag * amp_imag, axis=1)
    imag_part = jnp.sum(weight_real * amp_imag - weight_imag * amp_real, axis=1)
    return jnp.stack([real_part, imag_part], axis=1)


def shards(cell_spectra, cell_weight, cell_owner, cell_local, panel_position, observer_position):
    cell_rows, columns = cell_spectra.shape
    freqs_dev = columns // 8
    groups = lax.axis_size("obs")
    panel_total = panel_position.shape[1]
    panels_dev = panel_total // groups
    observers_dev = observer_position.shape[1]
    weighted = (cell_weight[:, None] * cell_spectra.astype(jnp.float32)).astype(jnp.bfloat16)
    panel_index = cell_owner[:, 0] * panels_dev + cell_local
    selector = (
        jnp.arange(panel_total, dtype=jnp.int32)[:, None] == panel_index[None, :]
    ).astype(jnp.bfloat16)
    local_source = jnp.dot(selector, weighted, preferred_element_type=jnp.float32)
    group_first = lax.axis_index("freq") * freqs_dev
    wave_numbers = wave_step * (
        (group_first + jnp.arange(freqs_dev, dtype=jnp.int32)).astype(jnp.float32) + 1.0
    )
    start_value = jnp.zeros((freqs_dev, 2, observers_dev), jnp.float32)
    arrived = lax.all_to_all(
        local_source.reshape(groups, panels_dev, columns), "obs", 0, 0, tiled=True
    )
    own_source = jnp.sum(arrived, axis=0)
    portion = lax.all_to_all(
        jnp.broadcast_to(own_source[None], (groups, panels_dev, columns)), "obs", 0, 0, tiled=True
    ).reshape(panel_total, columns)
    rows_count = portion.shape[0]
    tile_rows = math.gcd(rows_count, 256)

    def advance(turn, accum):
        source = lax.dynamic_slice_in_dim(portion, turn * tile_rows, tile_rows, 0).reshape(
            tile_rows, freqs_dev, 8
        )
        points = lax.dynamic_slice_in_dim(panel_position, turn * tile_rows, tile_rows, 1)
        return accum + kernel_block(source, points, observer_position, wave_numbers)

    summed = lax.fori_loop(0, rows_count // tile_rows, advance, start_value)
    pressure = summed * (reference_radius / math.sqrt(panel_total))
    energy = jnp.sum(pressure[:, 0] * pressure[:, 0] + pressure[:, 1] * pressure[:, 1], axis=0)
    if lax.axis_size("freq") == 2:
        band_total = energy + lax.ppermute(energy, "freq", [(0, 1), (1, 0)])
    else:
        band_total = lax.psum(energy, "freq")
    level = jnp.log(band_total / (freqs_dev * lax.axis_size("freq")) + 1e-06)
    return (pressure, level)


def solution(mesh):
    in_specs = (P("obs", "freq"), P("obs"), P("obs", None), P("obs"), P(), P(None, "obs"))
    out_specs = (P("freq", None, "obs"), P("obs"))
    return jax.shard_map(shards, mesh=mesh, in_specs=in_specs, out_specs=out_specs, check_vma=False)
```

```python
import math

import jax
import jax.numpy as jnp
from jax import lax
from jax.experimental import pallas as pl
from jax.experimental.pallas import tpu as pltpu
from jax.sharding import PartitionSpec as P

wave_step = 0.1
reference_radius = 10.0


def field_kernel(wave_ref, geo_ref, src_ref, out_ref):
    freqs = src_ref.shape[0]
    blocks = geo_ref.shape[1] // 8

    @pl.when(pl.program_id(0) == 0)
    def _():
        out_ref[...] = jnp.zeros(out_ref.shape, out_ref.dtype)

    def block_body(block, carry):
        rows = pl.ds(pl.multiple_of(block * 8, 8), 8)
        step_cos = geo_ref[2, rows, :]
        step_sin = geo_ref[3, rows, :]
        along = [geo_ref[4 + j, rows, :] for j in range(3)]
        distance = geo_ref[7, rows, :]

        def freq_body(f, phase):
            weight_real, weight_imag = phase
            channel = [jnp.broadcast_to(src_ref[f, c : c + 1, :], (8, 128)) for c in range(8)]
            wave_distance = wave_ref[f] * distance
            dipole_real = along[0] * channel[2] + along[1] * channel[4] + along[2] * channel[6]
            dipole_imag = along[0] * channel[3] + along[1] * channel[5] + along[2] * channel[7]
            amp_real = channel[0] + dipole_real - wave_distance * dipole_imag
            amp_imag = channel[1] + dipole_imag + wave_distance * dipole_real
            out_ref[f, 0, rows, :] += weight_real * amp_real + weight_imag * amp_imag
            out_ref[f, 1, rows, :] += weight_real * amp_imag - weight_imag * amp_real
            return (
                weight_real * step_cos - weight_imag * step_sin,
                weight_imag * step_cos + weight_real * step_sin,
            )

        lax.fori_loop(
            0, freqs, freq_body, (geo_ref[0, rows, :], geo_ref[1, rows, :]), unroll=2
        )
        return carry

    lax.fori_loop(0, blocks, block_body, 0)


def far_field(portion, panel_position, observer_position, wave_numbers):
    panel_total, columns = portion.shape
    freqs = columns // 8
    observers = observer_position.shape[1]
    offsets = observer_position[:, :, None] - panel_position[:, None, :]
    distance = jnp.sqrt(offsets[0] * offsets[0] + offsets[1] * offsets[1] + offsets[2] * offsets[2])
    inverse = 1.0 / distance
    first_phase = wave_numbers[0] * distance
    step_phase = wave_step * distance
    geometry = jnp.stack(
        [
            jnp.cos(first_phase) * inverse,
            jnp.sin(first_phase) * inverse,
            jnp.cos(step_phase),
            jnp.sin(step_phase),
            offsets[0] * inverse * inverse,
            offsets[1] * inverse * inverse,
            offsets[2] * inverse * inverse,
            distance,
        ]
    )
    sources = jnp.transpose(portion.reshape(panel_total, freqs, 8), (1, 2, 0))
    partial = pl.pallas_call(
        field_kernel,
        grid=(panel_total // 128,),
        in_specs=[
            pl.BlockSpec(memory_space=pltpu.SMEM),
            pl.BlockSpec((8, observers, 128), lambda chunk: (0, 0, chunk)),
            pl.BlockSpec((freqs, 8, 128), lambda chunk: (0, 0, chunk)),
        ],
        out_specs=pl.BlockSpec((freqs, 2, observers, 128), lambda chunk: (0, 0, 0, 0)),
        out_shape=jax.ShapeDtypeStruct((freqs, 2, observers, 128), jnp.float32),
        compiler_params=pltpu.CompilerParams(dimension_semantics=("arbitrary",)),
    )(wave_numbers, geometry, sources)
    return jnp.sum(partial, axis=-1)


def shards(cell_spectra, cell_weight, cell_owner, cell_local, panel_position, observer_position):
    cell_rows, columns = cell_spectra.shape
    freqs_dev = columns // 8
    groups = lax.axis_size("obs")
    panel_total = panel_position.shape[1]
    panels_dev = panel_total // groups
    weighted = (cell_weight[:, None] * cell_spectra.astype(jnp.float32)).astype(jnp.bfloat16)
    panel_index = cell_owner[:, 0] * panels_dev + cell_local
    selector = (
        jnp.arange(panel_total, dtype=jnp.int32)[:, None] == panel_index[None, :]
    ).astype(jnp.bfloat16)
    local_source = jnp.dot(selector, weighted, preferred_element_type=jnp.float32)
    group_first = lax.axis_index("freq") * freqs_dev
    wave_numbers = wave_step * (
        (group_first + jnp.arange(freqs_dev, dtype=jnp.int32)).astype(jnp.float32) + 1.0
    )
    arrived = lax.all_to_all(
        local_source.reshape(groups, panels_dev, columns), "obs", 0, 0, tiled=True
    )
    own_source = jnp.sum(arrived, axis=0)
    portion = lax.all_to_all(
        jnp.broadcast_to(own_source[None], (groups, panels_dev, columns)), "obs", 0, 0, tiled=True
    ).reshape(panel_total, columns)
    summed = far_field(portion, panel_position, observer_position, wave_numbers)
    pressure = summed * (reference_radius / math.sqrt(panel_total))
    energy = jnp.sum(pressure[:, 0] * pressure[:, 0] + pressure[:, 1] * pressure[:, 1], axis=0)
    if lax.axis_size("freq") == 2:
        band_total = energy + lax.ppermute(energy, "freq", [(0, 1), (1, 0)])
    else:
        band_total = lax.psum(energy, "freq")
    level = jnp.log(band_total / (freqs_dev * lax.axis_size("freq")) + 1e-06)
    return (pressure, level)


def solution(mesh):
    in_specs = (P("obs", "freq"), P("obs"), P("obs", None), P("obs"), P(), P(None, "obs"))
    out_specs = (P("freq", None, "obs"), P("obs"))
    return jax.shard_map(shards, mesh=mesh, in_specs=in_specs, out_specs=out_specs, check_vma=False)
```

```python
import math

import jax
import jax.numpy as jnp
from jax import lax
from jax.experimental import pallas as pl
from jax.experimental.pallas import tpu as pltpu
from jax.sharding import PartitionSpec as P

wave_step = 0.1
reference_radius = 10.0


def field_kernel(wave_ref, geo_ref, src_ref, out_ref, acc_ref, chan_ref):
    freqs, _, observers, lanes = acc_ref.shape
    blocks = observers // 8

    @pl.when(pl.program_id(0) == 0)
    def _():
        acc_ref[...] = jnp.zeros(acc_ref.shape, acc_ref.dtype)

    chan_ref[...] = jnp.transpose(src_ref[...])

    def block_body(block, carry):
        rows = pl.ds(pl.multiple_of(block * 8, 8), 8)
        step_cos = geo_ref[2, rows, :]
        step_sin = geo_ref[3, rows, :]
        along = [geo_ref[4 + j, rows, :] for j in range(3)]
        distance = geo_ref[7, rows, :]

        def freq_body(f, phase):
            weight_real, weight_imag = phase
            base = f * 8
            channel = [
                jnp.broadcast_to(chan_ref[pl.ds(base + c, 1), :], (8, lanes)) for c in range(8)
            ]
            wave_distance = wave_ref[f] * distance
            dipole_real = along[0] * channel[2] + along[1] * channel[4] + along[2] * channel[6]
            dipole_imag = along[0] * channel[3] + along[1] * channel[5] + along[2] * channel[7]
            amp_real = channel[0] + dipole_real - wave_distance * dipole_imag
            amp_imag = channel[1] + dipole_imag + wave_distance * dipole_real
            acc_ref[f, 0, rows, :] += weight_real * amp_real + weight_imag * amp_imag
            acc_ref[f, 1, rows, :] += weight_real * amp_imag - weight_imag * amp_real
            return (
                weight_real * step_cos - weight_imag * step_sin,
                weight_imag * step_cos + weight_real * step_sin,
            )

        lax.fori_loop(
            0, freqs, freq_body, (geo_ref[0, rows, :], geo_ref[1, rows, :]), unroll=2
        )
        return carry

    lax.fori_loop(0, blocks, block_body, 0)

    @pl.when(pl.program_id(0) == pl.num_programs(0) - 1)
    def _():
        flat = acc_ref[...].reshape(freqs * 2 * observers, lanes)
        out_ref[...] = lax.dot_general(
            jnp.ones((8, lanes), jnp.float32),
            flat,
            (((1,), (1,)), ((), ())),
            precision=lax.Precision.HIGHEST,
            preferred_element_type=jnp.float32,
        )


def far_field(portion, panel_position, observer_position, wave_numbers):
    panel_total, columns = portion.shape
    freqs = columns // 8
    observers = observer_position.shape[1]
    offsets = observer_position[:, :, None] - panel_position[:, None, :]
    distance = jnp.sqrt(offsets[0] * offsets[0] + offsets[1] * offsets[1] + offsets[2] * offsets[2])
    inverse = 1.0 / distance
    first_phase = wave_numbers[0] * distance
    step_phase = wave_step * distance
    geometry = jnp.stack(
        [
            jnp.cos(first_phase) * inverse,
            jnp.sin(first_phase) * inverse,
            jnp.cos(step_phase),
            jnp.sin(step_phase),
            offsets[0] * inverse * inverse,
            offsets[1] * inverse * inverse,
            offsets[2] * inverse * inverse,
            distance,
        ]
    )
    summed = pl.pallas_call(
        field_kernel,
        grid=(panel_total // 128,),
        in_specs=[
            pl.BlockSpec(memory_space=pltpu.SMEM),
            pl.BlockSpec((8, observers, 128), lambda chunk: (0, 0, chunk)),
            pl.BlockSpec((128, columns), lambda chunk: (chunk, 0)),
        ],
        out_specs=pl.BlockSpec((8, freqs * 2 * observers), lambda chunk: (0, 0)),
        out_shape=jax.ShapeDtypeStruct((8, freqs * 2 * observers), jnp.float32),
        scratch_shapes=[
            pltpu.VMEM((freqs, 2, observers, 128), jnp.float32),
            pltpu.VMEM((columns, 128), jnp.float32),
        ],
        compiler_params=pltpu.CompilerParams(dimension_semantics=("arbitrary",)),
    )(wave_numbers, geometry, portion)
    return summed[0].reshape(freqs, 2, observers)


def shards(cell_spectra, cell_weight, cell_owner, cell_local, panel_position, observer_position):
    cell_rows, columns = cell_spectra.shape
    freqs_dev = columns // 8
    groups = lax.axis_size("obs")
    panel_total = panel_position.shape[1]
    panels_dev = panel_total // groups
    weighted = (cell_weight[:, None] * cell_spectra.astype(jnp.float32)).astype(jnp.bfloat16)
    panel_number = jnp.arange(panel_total, dtype=jnp.int32)[:, None]
    selector = (
        (panel_number // panels_dev == cell_owner[:, 0][None, :])
        & (panel_number % panels_dev == cell_local[None, :])
    ).astype(jnp.bfloat16)
    local_source = jnp.dot(selector, weighted, preferred_element_type=jnp.float32)
    group_first = lax.axis_index("freq") * freqs_dev
    wave_numbers = wave_step * (
        (group_first + jnp.arange(freqs_dev, dtype=jnp.int32)).astype(jnp.float32) + 1.0
    )
    arrived = lax.all_to_all(
        local_source.reshape(groups, panels_dev, columns), "obs", 0, 0, tiled=True
    )
    own_source = jnp.sum(arrived, axis=0)
    portion = lax.all_to_all(
        jnp.broadcast_to(own_source[None], (groups, panels_dev, columns)), "obs", 0, 0, tiled=True
    ).reshape(panel_total, columns)
    summed = far_field(portion, panel_position, observer_position, wave_numbers)
    pressure = summed * (reference_radius / math.sqrt(panel_total))
    energy = jnp.sum(pressure[:, 0] * pressure[:, 0] + pressure[:, 1] * pressure[:, 1], axis=0)
    if lax.axis_size("freq") == 2:
        band_total = energy + lax.ppermute(energy, "freq", [(0, 1), (1, 0)])
    else:
        band_total = lax.psum(energy, "freq")
    level = jnp.log(band_total / (freqs_dev * lax.axis_size("freq")) + 1e-06)
    return (pressure, level)


def solution(mesh):
    in_specs = (P("obs", "freq"), P("obs"), P("obs", None), P("obs"), P(), P(None, "obs"))
    out_specs = (P("freq", None, "obs"), P("obs"))
    return jax.shard_map(shards, mesh=mesh, in_specs=in_specs, out_specs=out_specs, check_vma=False)
```

```python
import math

import jax
import jax.numpy as jnp
from jax import lax
from jax.experimental import pallas as pl
from jax.experimental.pallas import tpu as pltpu
from jax.sharding import PartitionSpec as P

wave_step = 0.1
reference_radius = 10.0


def field_kernel(wave_ref, geo_ref, src_ref, out_ref, acc_ref, chan_ref, spread_ref):
    freqs, _, observers, lanes = acc_ref.shape
    blocks = observers // 8

    @pl.when(pl.program_id(0) == 0)
    def _():
        acc_ref[...] = jnp.zeros(acc_ref.shape, acc_ref.dtype)

    chan_ref[...] = jnp.transpose(src_ref[...])

    def spread_body(row, carry):
        spread_ref[row] = jnp.broadcast_to(chan_ref[pl.ds(row, 1), :], (8, lanes))
        return carry

    lax.fori_loop(0, chan_ref.shape[0], spread_body, 0, unroll=8)

    def block_body(block, carry):
        rows = pl.ds(pl.multiple_of(block * 8, 8), 8)
        step_cos = geo_ref[2, rows, :]
        step_sin = geo_ref[3, rows, :]
        along = [geo_ref[4 + j, rows, :] for j in range(3)]
        distance = geo_ref[7, rows, :]

        def freq_body(f, phase):
            weight_real, weight_imag = phase
            base = f * 8
            channel = [spread_ref[base + c] for c in range(8)]
            wave_distance = wave_ref[f] * distance
            dipole_real = along[0] * channel[2] + along[1] * channel[4] + along[2] * channel[6]
            dipole_imag = along[0] * channel[3] + along[1] * channel[5] + along[2] * channel[7]
            amp_real = channel[0] + dipole_real - wave_distance * dipole_imag
            amp_imag = channel[1] + dipole_imag + wave_distance * dipole_real
            acc_ref[f, 0, rows, :] += weight_real * amp_real + weight_imag * amp_imag
            acc_ref[f, 1, rows, :] += weight_real * amp_imag - weight_imag * amp_real
            return (
                weight_real * step_cos - weight_imag * step_sin,
                weight_imag * step_cos + weight_real * step_sin,
            )

        lax.fori_loop(
            0, freqs, freq_body, (geo_ref[0, rows, :], geo_ref[1, rows, :]), unroll=4
        )
        return carry

    lax.fori_loop(0, blocks, block_body, 0)

    @pl.when(pl.program_id(0) == pl.num_programs(0) - 1)
    def _():
        flat = acc_ref[...].reshape(freqs * 2 * observers, lanes)
        out_ref[...] = lax.dot_general(
            jnp.ones((8, lanes), jnp.float32),
            flat,
            (((1,), (1,)), ((), ())),
            precision=lax.Precision.HIGHEST,
            preferred_element_type=jnp.float32,
        )


def far_field(portion, panel_position, observer_position, wave_numbers):
    panel_total, columns = portion.shape
    freqs = columns // 8
    observers = observer_position.shape[1]
    offsets = observer_position[:, :, None] - panel_position[:, None, :]
    distance = jnp.sqrt(offsets[0] * offsets[0] + offsets[1] * offsets[1] + offsets[2] * offsets[2])
    inverse = 1.0 / distance
    first_phase = wave_numbers[0] * distance
    step_phase = wave_step * distance
    geometry = jnp.stack(
        [
            jnp.cos(first_phase) * inverse,
            jnp.sin(first_phase) * inverse,
            jnp.cos(step_phase),
            jnp.sin(step_phase),
            offsets[0] * inverse * inverse,
            offsets[1] * inverse * inverse,
            offsets[2] * inverse * inverse,
            distance,
        ]
    )
    summed = pl.pallas_call(
        field_kernel,
        grid=(panel_total // 128,),
        in_specs=[
            pl.BlockSpec(memory_space=pltpu.SMEM),
            pl.BlockSpec((8, observers, 128), lambda chunk: (0, 0, chunk)),
            pl.BlockSpec((128, columns), lambda chunk: (chunk, 0)),
        ],
        out_specs=pl.BlockSpec((8, freqs * 2 * observers), lambda chunk: (0, 0)),
        out_shape=jax.ShapeDtypeStruct((8, freqs * 2 * observers), jnp.float32),
        scratch_shapes=[
            pltpu.VMEM((freqs, 2, observers, 128), jnp.float32),
            pltpu.VMEM((columns, 128), jnp.float32),
            pltpu.VMEM((columns, 8, 128), jnp.float32),
        ],
        compiler_params=pltpu.CompilerParams(dimension_semantics=("arbitrary",)),
    )(wave_numbers, geometry, portion)
    return summed[0].reshape(freqs, 2, observers)


def shards(cell_spectra, cell_weight, cell_owner, cell_local, panel_position, observer_position):
    cell_rows, columns = cell_spectra.shape
    freqs_dev = columns // 8
    groups = lax.axis_size("obs")
    panel_total = panel_position.shape[1]
    panels_dev = panel_total // groups
    weighted = (cell_weight[:, None] * cell_spectra.astype(jnp.float32)).astype(jnp.bfloat16)
    panel_number = jnp.arange(panel_total, dtype=jnp.int32)[:, None]
    selector = (
        (panel_number // panels_dev == cell_owner[:, 0][None, :])
        & (panel_number % panels_dev == cell_local[None, :])
    ).astype(jnp.bfloat16)
    local_source = jnp.dot(selector, weighted, preferred_element_type=jnp.float32)
    group_first = lax.axis_index("freq") * freqs_dev
    wave_numbers = wave_step * (
        (group_first + jnp.arange(freqs_dev, dtype=jnp.int32)).astype(jnp.float32) + 1.0
    )
    arrived = lax.all_to_all(
        local_source.reshape(groups, panels_dev, columns), "obs", 0, 0, tiled=True
    )
    own_source = jnp.sum(arrived, axis=0)
    portion = lax.all_to_all(
        jnp.broadcast_to(own_source[None], (groups, panels_dev, columns)), "obs", 0, 0, tiled=True
    ).reshape(panel_total, columns)
    summed = far_field(portion, panel_position, observer_position, wave_numbers)
    pressure = summed * (reference_radius / math.sqrt(panel_total))
    energy = jnp.sum(pressure[:, 0] * pressure[:, 0] + pressure[:, 1] * pressure[:, 1], axis=0)
    if lax.axis_size("freq") == 2:
        band_total = energy + lax.ppermute(energy, "freq", [(0, 1), (1, 0)])
    else:
        band_total = lax.psum(energy, "freq")
    level = jnp.log(band_total / (freqs_dev * lax.axis_size("freq")) + 1e-06)
    return (pressure, level)


def solution(mesh):
    in_specs = (P("obs", "freq"), P("obs"), P("obs", None), P("obs"), P(), P(None, "obs"))
    out_specs = (P("freq", None, "obs"), P("obs"))
    return jax.shard_map(shards, mesh=mesh, in_specs=in_specs, out_specs=out_specs, check_vma=False)
```

```python
import functools
import math

import jax
import jax.numpy as jnp
from jax import lax
from jax.experimental import pallas as pl
from jax.experimental.pallas import tpu as pltpu
from jax.sharding import PartitionSpec as P

wave_step = 0.1
reference_radius = 10.0


def field_kernel(block_group, freq_unroll, wave_ref, geo_ref, src_ref, out_ref, acc_ref, chan_ref, spread_ref):
    freqs, _, observers, lanes = acc_ref.shape
    blocks = observers // 8

    @pl.when(pl.program_id(0) == 0)
    def _():
        acc_ref[...] = jnp.zeros(acc_ref.shape, acc_ref.dtype)

    chan_ref[...] = jnp.transpose(src_ref[...])

    def spread_body(row, carry):
        spread_ref[row] = jnp.broadcast_to(chan_ref[pl.ds(row, 1), :], (8, lanes))
        return carry

    lax.fori_loop(0, chan_ref.shape[0], spread_body, 0, unroll=8)

    def block_body(group, carry):
        spans = [
            pl.ds(pl.multiple_of((group * block_group + member) * 8, 8), 8)
            for member in range(block_group)
        ]
        step_cos = [geo_ref[2, rows, :] for rows in spans]
        step_sin = [geo_ref[3, rows, :] for rows in spans]
        along = [[geo_ref[4 + j, rows, :] for j in range(3)] for rows in spans]
        distance = [geo_ref[7, rows, :] for rows in spans]

        def freq_body(f, phase):
            base = f * 8
            channel = [spread_ref[base + c] for c in range(8)]
            wave = wave_ref[f]
            turned = []
            for member, rows in enumerate(spans):
                weight_real, weight_imag = phase[member]
                g = along[member]
                wave_distance = wave * distance[member]
                dipole_real = g[0] * channel[2] + g[1] * channel[4] + g[2] * channel[6]
                dipole_imag = g[0] * channel[3] + g[1] * channel[5] + g[2] * channel[7]
                amp_real = channel[0] + dipole_real - wave_distance * dipole_imag
                amp_imag = channel[1] + dipole_imag + wave_distance * dipole_real
                acc_ref[f, 0, rows, :] += weight_real * amp_real + weight_imag * amp_imag
                acc_ref[f, 1, rows, :] += weight_real * amp_imag - weight_imag * amp_real
                turned.append(
                    (
                        weight_real * step_cos[member] - weight_imag * step_sin[member],
                        weight_imag * step_cos[member] + weight_real * step_sin[member],
                    )
                )
            return tuple(turned)

        start = tuple((geo_ref[0, rows, :], geo_ref[1, rows, :]) for rows in spans)
        lax.fori_loop(0, freqs, freq_body, start, unroll=freq_unroll)
        return carry

    lax.fori_loop(0, blocks // block_group, block_body, 0)

    @pl.when(pl.program_id(0) == pl.num_programs(0) - 1)
    def _():
        flat = acc_ref[...].reshape(freqs * 2 * observers, lanes)
        out_ref[...] = lax.dot_general(
            jnp.ones((8, lanes), jnp.float32),
            flat,
            (((1,), (1,)), ((), ())),
            precision=lax.Precision.HIGHEST,
            preferred_element_type=jnp.float32,
        )


def far_field(portion, panel_position, observer_position, wave_numbers):
    panel_total, columns = portion.shape
    freqs = columns // 8
    observers = observer_position.shape[1]
    offsets = observer_position[:, :, None] - panel_position[:, None, :]
    distance = jnp.sqrt(offsets[0] * offsets[0] + offsets[1] * offsets[1] + offsets[2] * offsets[2])
    inverse = 1.0 / distance
    first_phase = wave_numbers[0] * distance
    step_phase = wave_step * distance
    geometry = jnp.stack(
        [
            jnp.cos(first_phase) * inverse,
            jnp.sin(first_phase) * inverse,
            jnp.cos(step_phase),
            jnp.sin(step_phase),
            offsets[0] * inverse * inverse,
            offsets[1] * inverse * inverse,
            offsets[2] * inverse * inverse,
            distance,
        ]
    )
    summed = pl.pallas_call(
        functools.partial(field_kernel, math.gcd(observers // 8, 4), 2),
        grid=(panel_total // 128,),
        in_specs=[
            pl.BlockSpec(memory_space=pltpu.SMEM),
            pl.BlockSpec((8, observers, 128), lambda chunk: (0, 0, chunk)),
            pl.BlockSpec((128, columns), lambda chunk: (chunk, 0)),
        ],
        out_specs=pl.BlockSpec((8, freqs * 2 * observers), lambda chunk: (0, 0)),
        out_shape=jax.ShapeDtypeStruct((8, freqs * 2 * observers), jnp.float32),
        scratch_shapes=[
            pltpu.VMEM((freqs, 2, observers, 128), jnp.float32),
            pltpu.VMEM((columns, 128), jnp.float32),
            pltpu.VMEM((columns, 8, 128), jnp.float32),
        ],
        compiler_params=pltpu.CompilerParams(dimension_semantics=("arbitrary",)),
    )(wave_numbers, geometry, portion)
    return summed[0].reshape(freqs, 2, observers)


def partner_pairs(groups, bit):
    return [(k, k ^ bit) for k in range(groups)]


def halving_sum(blocks, bits):
    groups = blocks.shape[0]
    place = lax.axis_index("obs")
    current = blocks
    for bit in bits:
        split = current.reshape((current.shape[0] // 2, 2) + current.shape[1:])
        mine = (place // bit) % 2
        keep = lax.dynamic_index_in_dim(split, mine, 1, keepdims=False)
        send = lax.dynamic_index_in_dim(split, 1 - mine, 1, keepdims=False)
        current = keep + lax.ppermute(send, "obs", partner_pairs(groups, bit))
    return current


def doubling_gather(own, bits, groups):
    place = lax.axis_index("obs")
    gathered = own
    for bit in reversed(bits):
        mine = (place // bit) % 2
        other = lax.ppermute(gathered, "obs", partner_pairs(groups, bit))
        low = jnp.where(mine == 0, gathered, other)
        high = jnp.where(mine == 0, other, gathered)
        gathered = jnp.stack([low, high], axis=1).reshape((-1,) + gathered.shape[1:])
    return gathered


def shards(cell_spectra, cell_weight, cell_owner, cell_local, panel_position, observer_position):
    cell_rows, columns = cell_spectra.shape
    freqs_dev = columns // 8
    groups = lax.axis_size("obs")
    panel_total = panel_position.shape[1]
    panels_dev = panel_total // groups
    weighted = (cell_weight[:, None] * cell_spectra.astype(jnp.float32)).astype(jnp.bfloat16)
    panel_number = jnp.arange(panel_total, dtype=jnp.int32)[:, None]
    selector = (
        (panel_number // panels_dev == cell_owner[:, 0][None, :])
        & (panel_number % panels_dev == cell_local[None, :])
    ).astype(jnp.bfloat16)
    local_source = jnp.dot(selector, weighted, preferred_element_type=jnp.float32)
    group_first = lax.axis_index("freq") * freqs_dev
    wave_numbers = wave_step * (
        (group_first + jnp.arange(freqs_dev, dtype=jnp.int32)).astype(jnp.float32) + 1.0
    )
    blocks = local_source.reshape(groups, panels_dev, columns)
    if groups & (groups - 1) == 0:
        bits = [1 << k for k in range(groups.bit_length() - 1)]
        own_source = halving_sum(blocks, bits)
        portion = doubling_gather(own_source, bits, groups).reshape(panel_total, columns)
    else:
        own_source = jnp.sum(lax.all_to_all(blocks, "obs", 0, 0, tiled=True), axis=0)
        portion = lax.all_to_all(
            jnp.broadcast_to(own_source[None], blocks.shape), "obs", 0, 0, tiled=True
        ).reshape(panel_total, columns)
    summed = far_field(portion, panel_position, observer_position, wave_numbers)
    pressure = summed * (reference_radius / math.sqrt(panel_total))
    energy = jnp.sum(pressure[:, 0] * pressure[:, 0] + pressure[:, 1] * pressure[:, 1], axis=0)
    if lax.axis_size("freq") == 2:
        band_total = energy + lax.ppermute(energy, "freq", [(0, 1), (1, 0)])
    else:
        band_total = lax.psum(energy, "freq")
    level = jnp.log(band_total / (freqs_dev * lax.axis_size("freq")) + 1e-06)
    return (pressure, level)


def solution(mesh):
    in_specs = (P("obs", "freq"), P("obs"), P("obs", None), P("obs"), P(), P(None, "obs"))
    out_specs = (P("freq", None, "obs"), P("obs"))
    return jax.shard_map(shards, mesh=mesh, in_specs=in_specs, out_specs=out_specs, check_vma=False)
```

```python
import functools
import math

import jax
import jax.numpy as jnp
from jax import lax
from jax.experimental import pallas as pl
from jax.experimental.pallas import tpu as pltpu
from jax.sharding import PartitionSpec as P

wave_step = 0.1
reference_radius = 10.0


def field_kernel(
    block_group, freq_unroll, scale, low_chunks, wave_ref, geo_ref, low_ref, high_ref, out_ref, acc_ref, chan_ref, spread_ref
):
    freqs, _, observers, lanes = acc_ref.shape
    blocks = observers // 8

    @pl.when(pl.program_id(0) == 0)
    def _():
        acc_ref[...] = jnp.zeros(acc_ref.shape, acc_ref.dtype)

    chunk = pl.program_id(0)

    @pl.when(chunk < low_chunks)
    def _():
        chan_ref[...] = jnp.transpose(low_ref[...])

    @pl.when(chunk >= low_chunks)
    def _():
        chan_ref[...] = jnp.transpose(high_ref[...])

    def spread_body(row, carry):
        spread_ref[row] = jnp.broadcast_to(chan_ref[pl.ds(row, 1), :], (8, lanes))
        return carry

    lax.fori_loop(0, chan_ref.shape[0], spread_body, 0, unroll=8)

    def block_body(group, carry):
        spans = [
            pl.ds(pl.multiple_of((group * block_group + member) * 8, 8), 8)
            for member in range(block_group)
        ]
        step_cos = [geo_ref[2, rows, :] for rows in spans]
        step_sin = [geo_ref[3, rows, :] for rows in spans]
        along = [[geo_ref[4 + j, rows, :] for j in range(3)] for rows in spans]
        distance = [geo_ref[7, rows, :] for rows in spans]

        def freq_body(f, phase):
            base = f * 8
            channel = [spread_ref[base + c] for c in range(8)]
            wave = wave_ref[f]
            turned = []
            for member, rows in enumerate(spans):
                weight_real, weight_imag = phase[member]
                g = along[member]
                wave_distance = wave * distance[member]
                dipole_real = g[0] * channel[2] + g[1] * channel[4] + g[2] * channel[6]
                dipole_imag = g[0] * channel[3] + g[1] * channel[5] + g[2] * channel[7]
                amp_real = channel[0] + dipole_real - wave_distance * dipole_imag
                amp_imag = channel[1] + dipole_imag + wave_distance * dipole_real
                acc_ref[f, 0, rows, :] += weight_real * amp_real + weight_imag * amp_imag
                acc_ref[f, 1, rows, :] += weight_real * amp_imag - weight_imag * amp_real
                turned.append(
                    (
                        weight_real * step_cos[member] - weight_imag * step_sin[member],
                        weight_imag * step_cos[member] + weight_real * step_sin[member],
                    )
                )
            return tuple(turned)

        start = tuple((geo_ref[0, rows, :], geo_ref[1, rows, :]) for rows in spans)
        lax.fori_loop(0, freqs, freq_body, start, unroll=freq_unroll)
        return carry

    lax.fori_loop(0, blocks // block_group, block_body, 0)

    @pl.when(pl.program_id(0) == pl.num_programs(0) - 1)
    def _():
        flat = acc_ref[...].reshape(freqs * 2 * observers, lanes)
        summed = lax.dot_general(
            jnp.ones((8, lanes), jnp.float32),
            flat,
            (((1,), (1,)), ((), ())),
            precision=lax.Precision.HIGHEST,
            preferred_element_type=jnp.float32,
        )
        out_ref[...] = summed[0:1, :] * scale


def far_field(low, high, panel_position, observer_position, wave_numbers, scale):
    columns = low.shape[1]
    freqs = columns // 8
    observers = observer_position.shape[1]
    low_chunks = low.shape[0] // 128
    high_chunks = high.shape[0] // 128
    offsets = observer_position[:, :, None] - panel_position[:, None, :]
    distance = jnp.sqrt(offsets[0] * offsets[0] + offsets[1] * offsets[1] + offsets[2] * offsets[2])
    inverse = 1.0 / distance
    first_phase = wave_numbers[0] * distance
    step_phase = wave_step * distance
    geometry = jnp.stack(
        [
            jnp.cos(first_phase) * inverse,
            jnp.sin(first_phase) * inverse,
            jnp.cos(step_phase),
            jnp.sin(step_phase),
            offsets[0] * inverse * inverse,
            offsets[1] * inverse * inverse,
            offsets[2] * inverse * inverse,
            distance,
        ]
    )
    kernel = functools.partial(field_kernel, math.gcd(observers // 8, 4), 2, scale, low_chunks)
    summed = pl.pallas_call(
        kernel,
        grid=(low_chunks + high_chunks,),
        in_specs=[
            pl.BlockSpec(memory_space=pltpu.SMEM),
            pl.BlockSpec((8, observers, 128), lambda chunk: (0, 0, chunk)),
            pl.BlockSpec((128, columns), lambda chunk: (jnp.minimum(chunk, low_chunks - 1), 0)),
            pl.BlockSpec((128, columns), lambda chunk: (jnp.maximum(chunk - low_chunks, 0), 0)),
        ],
        out_specs=pl.BlockSpec((1, freqs * 2 * observers), lambda chunk: (0, 0)),
        out_shape=jax.ShapeDtypeStruct((1, freqs * 2 * observers), jnp.float32),
        scratch_shapes=[
            pltpu.VMEM((freqs, 2, observers, 128), jnp.float32),
            pltpu.VMEM((columns, 128), jnp.float32),
            pltpu.VMEM((columns, 8, 128), jnp.float32),
        ],
        compiler_params=pltpu.CompilerParams(dimension_semantics=("arbitrary",)),
    )(wave_numbers, geometry, low, high)
    return summed.reshape(freqs, 2, observers)


def partner_pairs(groups, bit):
    return [(k, k ^ bit) for k in range(groups)]


def halving_sum(blocks, bits):
    groups = blocks.shape[0]
    place = lax.axis_index("obs")
    current = blocks
    for bit in bits:
        split = current.reshape((current.shape[0] // 2, 2) + current.shape[1:])
        mine = (place // bit) % 2
        keep = lax.dynamic_index_in_dim(split, mine, 1, keepdims=False)
        send = lax.dynamic_index_in_dim(split, 1 - mine, 1, keepdims=False)
        current = keep + lax.ppermute(send, "obs", partner_pairs(groups, bit))
    return current


def doubling_gather(own, bits, groups):
    place = lax.axis_index("obs")
    gathered = own
    for bit in reversed(bits):
        mine = (place // bit) % 2
        other = lax.ppermute(gathered, "obs", partner_pairs(groups, bit))
        low = jnp.where(mine == 0, gathered, other)
        high = jnp.where(mine == 0, other, gathered)
        if bit == 1:
            return low, high
        gathered = jnp.stack([low, high], axis=1).reshape((-1,) + gathered.shape[1:])


def shards(cell_spectra, cell_weight, cell_owner, cell_local, panel_position, observer_position):
    cell_rows, columns = cell_spectra.shape
    freqs_dev = columns // 8
    groups = lax.axis_size("obs")
    panel_total = panel_position.shape[1]
    panels_dev = panel_total // groups
    weighted = (cell_weight[:, None] * cell_spectra.astype(jnp.float32)).astype(jnp.bfloat16)
    panel_number = jnp.arange(panel_total, dtype=jnp.int32)[:, None]
    selector = (
        (panel_number // panels_dev == cell_owner[:, 0][None, :])
        & (panel_number % panels_dev == cell_local[None, :])
    ).astype(jnp.bfloat16)
    local_source = jnp.dot(selector, weighted, preferred_element_type=jnp.float32)
    group_first = lax.axis_index("freq") * freqs_dev
    wave_numbers = wave_step * (
        (group_first + jnp.arange(freqs_dev, dtype=jnp.int32)).astype(jnp.float32) + 1.0
    )
    blocks = local_source.reshape(groups, panels_dev, columns)
    scale = reference_radius / math.sqrt(panel_total)
    if groups & (groups - 1) == 0 and groups >= 8:
        bits = [1 << k for k in range(groups.bit_length() - 1)]
        own_source = halving_sum(blocks, bits)
        even, odd = doubling_gather(own_source, bits, groups)
        order = jnp.transpose(panel_position.reshape(3, groups // 2, 2, panels_dev), (0, 2, 1, 3))
        pressure = far_field(
            even.reshape(-1, columns),
            odd.reshape(-1, columns),
            order.reshape(3, panel_total),
            observer_position,
            wave_numbers,
            scale,
        )
    else:
        own_source = jnp.sum(lax.all_to_all(blocks, "obs", 0, 0, tiled=True), axis=0)
        portion = lax.all_to_all(
            jnp.broadcast_to(own_source[None], blocks.shape), "obs", 0, 0, tiled=True
        ).reshape(panel_total, columns)
        half = panel_total // 256 * 128
        pressure = far_field(
            portion[:half], portion[half:], panel_position, observer_position, wave_numbers, scale
        )
    energy = jnp.sum(pressure[:, 0] * pressure[:, 0] + pressure[:, 1] * pressure[:, 1], axis=0)
    if lax.axis_size("freq") == 2:
        band_total = energy + lax.ppermute(energy, "freq", [(0, 1), (1, 0)])
    else:
        band_total = lax.psum(energy, "freq")
    level = jnp.log(band_total / (freqs_dev * lax.axis_size("freq")) + 1e-06)
    return (pressure, level)


def solution(mesh):
    in_specs = (P("obs", "freq"), P("obs"), P("obs", None), P("obs"), P(), P(None, "obs"))
    out_specs = (P("freq", None, "obs"), P("obs"))
    return jax.shard_map(shards, mesh=mesh, in_specs=in_specs, out_specs=out_specs, check_vma=False)
```

```python
import functools
import math

import jax
import jax.numpy as jnp
from jax import lax
from jax.experimental import pallas as pl
from jax.experimental.pallas import tpu as pltpu
from jax.sharding import PartitionSpec as P

wave_step = 0.1
reference_radius = 10.0


def field_kernel(block_group, freq_unroll, wave_ref, geo_ref, src_ref, out_ref, acc_ref, chan_ref, spread_ref):
    freqs, _, observers, lanes = acc_ref.shape
    blocks = observers // 8

    @pl.when(pl.program_id(0) == 0)
    def _():
        acc_ref[...] = jnp.zeros(acc_ref.shape, acc_ref.dtype)

    chan_ref[...] = jnp.transpose(src_ref[...])

    def spread_body(row, carry):
        spread_ref[row] = jnp.broadcast_to(chan_ref[pl.ds(row, 1), :], (8, lanes))
        return carry

    lax.fori_loop(0, chan_ref.shape[0], spread_body, 0, unroll=8)

    def block_body(group, carry):
        spans = [
            pl.ds(pl.multiple_of((group * block_group + member) * 8, 8), 8)
            for member in range(block_group)
        ]
        step_cos = [geo_ref[2, rows, :] for rows in spans]
        step_sin = [geo_ref[3, rows, :] for rows in spans]
        along = [[geo_ref[4 + j, rows, :] for j in range(3)] for rows in spans]
        distance = [geo_ref[7, rows, :] for rows in spans]

        def freq_body(f, phase):
            base = f * 8
            channel = [spread_ref[base + c] for c in range(8)]
            wave = wave_ref[f]
            turned = []
            for member, rows in enumerate(spans):
                weight_real, weight_imag = phase[member]
                g = along[member]
                wave_distance = wave * distance[member]
                dipole_real = g[0] * channel[2] + g[1] * channel[4] + g[2] * channel[6]
                dipole_imag = g[0] * channel[3] + g[1] * channel[5] + g[2] * channel[7]
                amp_real = channel[0] + dipole_real - wave_distance * dipole_imag
                amp_imag = channel[1] + dipole_imag + wave_distance * dipole_real
                acc_ref[f, 0, rows, :] += weight_real * amp_real + weight_imag * amp_imag
                acc_ref[f, 1, rows, :] += weight_real * amp_imag - weight_imag * amp_real
                turned.append(
                    (
                        weight_real * step_cos[member] - weight_imag * step_sin[member],
                        weight_imag * step_cos[member] + weight_real * step_sin[member],
                    )
                )
            return tuple(turned)

        start = tuple((geo_ref[0, rows, :], geo_ref[1, rows, :]) for rows in spans)
        lax.fori_loop(0, freqs, freq_body, start, unroll=freq_unroll)
        return carry

    lax.fori_loop(0, blocks // block_group, block_body, 0)

    @pl.when(pl.program_id(0) == pl.num_programs(0) - 1)
    def _():
        flat = acc_ref[...].reshape(freqs * 2 * observers, lanes)
        out_ref[...] = lax.dot_general(
            jnp.ones((8, lanes), jnp.float32),
            flat,
            (((1,), (1,)), ((), ())),
            precision=lax.Precision.HIGHEST,
            preferred_element_type=jnp.float32,
        )


def far_field(portion, panel_position, observer_position, wave_numbers):
    panel_total, columns = portion.shape
    freqs = columns // 8
    observers = observer_position.shape[1]
    offsets = observer_position[:, :, None] - panel_position[:, None, :]
    distance = jnp.sqrt(offsets[0] * offsets[0] + offsets[1] * offsets[1] + offsets[2] * offsets[2])
    inverse = 1.0 / distance
    first_phase = wave_numbers[0] * distance
    step_phase = wave_step * distance
    geometry = jnp.stack(
        [
            jnp.cos(first_phase) * inverse,
            jnp.sin(first_phase) * inverse,
            jnp.cos(step_phase),
            jnp.sin(step_phase),
            offsets[0] * inverse * inverse,
            offsets[1] * inverse * inverse,
            offsets[2] * inverse * inverse,
            distance,
        ]
    )
    summed = pl.pallas_call(
        functools.partial(field_kernel, math.gcd(observers // 8, 4), 2),
        grid=(panel_total // 128,),
        in_specs=[
            pl.BlockSpec(memory_space=pltpu.SMEM),
            pl.BlockSpec((8, observers, 128), lambda chunk: (0, 0, chunk)),
            pl.BlockSpec((128, columns), lambda chunk: (chunk, 0)),
        ],
        out_specs=pl.BlockSpec((8, freqs * 2 * observers), lambda chunk: (0, 0)),
        out_shape=jax.ShapeDtypeStruct((8, freqs * 2 * observers), jnp.float32),
        scratch_shapes=[
            pltpu.VMEM((freqs, 2, observers, 128), jnp.float32),
            pltpu.VMEM((columns, 128), jnp.float32),
            pltpu.VMEM((columns, 8, 128), jnp.float32),
        ],
        compiler_params=pltpu.CompilerParams(dimension_semantics=("arbitrary",)),
    )(wave_numbers, geometry, portion)
    return summed[0].reshape(freqs, 2, observers)


def partner_pairs(groups, bit):
    return [(k, k ^ bit) for k in range(groups)]


def quad_pairs(groups, shift):
    low = groups // 4
    return [(k, ((k // low + shift) % 4) * low + k % low) for k in range(groups)]


def halving_sum(blocks, bits):
    groups = blocks.shape[0]
    place = lax.axis_index("obs")
    current = blocks
    for bit in bits:
        split = current.reshape((current.shape[0] // 2, 2) + current.shape[1:])
        mine = (place // bit) % 2
        keep = lax.dynamic_index_in_dim(split, mine, 1, keepdims=False)
        send = lax.dynamic_index_in_dim(split, 1 - mine, 1, keepdims=False)
        current = keep + lax.ppermute(send, "obs", partner_pairs(groups, bit))
    quarter = place // (groups // 4)
    total = lax.dynamic_index_in_dim(current, quarter, 0, keepdims=False)
    for shift in (1, 2, 3):
        piece = lax.dynamic_index_in_dim(current, (quarter + shift) % 4, 0, keepdims=False)
        total = total + lax.ppermute(piece, "obs", quad_pairs(groups, shift))
    return total


def doubling_gather(own, bits, groups):
    place = lax.axis_index("obs")
    quarter = place // (groups // 4)
    arrived = jnp.stack(
        [own] + [lax.ppermute(own, "obs", quad_pairs(groups, shift)) for shift in (1, 2, 3)]
    )
    gathered = jnp.stack(
        [lax.dynamic_index_in_dim(arrived, (quarter - k) % 4, 0, keepdims=False) for k in range(4)]
    )
    for bit in reversed(bits):
        mine = (place // bit) % 2
        other = lax.ppermute(gathered, "obs", partner_pairs(groups, bit))
        low = jnp.where(mine == 0, gathered, other)
        high = jnp.where(mine == 0, other, gathered)
        gathered = jnp.stack([low, high], axis=1).reshape((-1,) + gathered.shape[1:])
    return gathered


def shards(cell_spectra, cell_weight, cell_owner, cell_local, panel_position, observer_position):
    cell_rows, columns = cell_spectra.shape
    freqs_dev = columns // 8
    groups = lax.axis_size("obs")
    panel_total = panel_position.shape[1]
    panels_dev = panel_total // groups
    weighted = (cell_weight[:, None] * cell_spectra.astype(jnp.float32)).astype(jnp.bfloat16)
    panel_number = jnp.arange(panel_total, dtype=jnp.int32)[:, None]
    selector = (
        (panel_number // panels_dev == cell_owner[:, 0][None, :])
        & (panel_number % panels_dev == cell_local[None, :])
    ).astype(jnp.bfloat16)
    local_source = jnp.dot(selector, weighted, preferred_element_type=jnp.float32)
    group_first = lax.axis_index("freq") * freqs_dev
    wave_numbers = wave_step * (
        (group_first + jnp.arange(freqs_dev, dtype=jnp.int32)).astype(jnp.float32) + 1.0
    )
    blocks = local_source.reshape(groups, panels_dev, columns)
    if groups & (groups - 1) == 0 and groups >= 4:
        bits = [1 << k for k in range(groups.bit_length() - 3)]
        own_source = halving_sum(blocks, bits)
        portion = doubling_gather(own_source, bits, groups).reshape(panel_total, columns)
    else:
        own_source = jnp.sum(lax.all_to_all(blocks, "obs", 0, 0, tiled=True), axis=0)
        portion = lax.all_to_all(
            jnp.broadcast_to(own_source[None], blocks.shape), "obs", 0, 0, tiled=True
        ).reshape(panel_total, columns)
    summed = far_field(portion, panel_position, observer_position, wave_numbers)
    pressure = summed * (reference_radius / math.sqrt(panel_total))
    energy = jnp.sum(pressure[:, 0] * pressure[:, 0] + pressure[:, 1] * pressure[:, 1], axis=0)
    if lax.axis_size("freq") == 2:
        band_total = energy + lax.ppermute(energy, "freq", [(0, 1), (1, 0)])
    else:
        band_total = lax.psum(energy, "freq")
    level = jnp.log(band_total / (freqs_dev * lax.axis_size("freq")) + 1e-06)
    return (pressure, level)


def solution(mesh):
    in_specs = (P("obs", "freq"), P("obs"), P("obs", None), P("obs"), P(), P(None, "obs"))
    out_specs = (P("freq", None, "obs"), P("obs"))
    return jax.shard_map(shards, mesh=mesh, in_specs=in_specs, out_specs=out_specs, check_vma=False)
```

```python
import functools
import math

import jax
import jax.numpy as jnp
from jax import lax
from jax.experimental import pallas as pl
from jax.experimental.pallas import tpu as pltpu
from jax.sharding import PartitionSpec as P

wave_step = 0.1
reference_radius = 10.0


def field_kernel(
    block_group, freq_unroll, chunk_ref, wave_ref, geo_ref, src_ref, out_ref, acc_ref, chan_ref, spread_ref
):
    freqs, _, observers, lanes = acc_ref.shape
    blocks = observers // 8

    @pl.when(pl.program_id(0) == 0)
    def _():
        acc_ref[...] = jnp.zeros(acc_ref.shape, acc_ref.dtype)

    chan_ref[...] = jnp.transpose(src_ref[...])

    def spread_body(row, carry):
        spread_ref[row] = jnp.broadcast_to(chan_ref[pl.ds(row, 1), :], (8, lanes))
        return carry

    lax.fori_loop(0, chan_ref.shape[0], spread_body, 0, unroll=8)

    def block_body(group, carry):
        spans = [
            pl.ds(pl.multiple_of((group * block_group + member) * 8, 8), 8)
            for member in range(block_group)
        ]
        step_cos = [geo_ref[2, rows, :] for rows in spans]
        step_sin = [geo_ref[3, rows, :] for rows in spans]
        along = [[geo_ref[4 + j, rows, :] for j in range(3)] for rows in spans]
        distance = [geo_ref[7, rows, :] for rows in spans]

        def freq_body(f, phase):
            base = f * 8
            channel = [spread_ref[base + c] for c in range(8)]
            wave = wave_ref[f]
            turned = []
            for member, rows in enumerate(spans):
                weight_real, weight_imag = phase[member]
                g = along[member]
                wave_distance = wave * distance[member]
                dipole_real = g[0] * channel[2] + g[1] * channel[4] + g[2] * channel[6]
                dipole_imag = g[0] * channel[3] + g[1] * channel[5] + g[2] * channel[7]
                amp_real = channel[0] + dipole_real - wave_distance * dipole_imag
                amp_imag = channel[1] + dipole_imag + wave_distance * dipole_real
                acc_ref[f, 0, rows, :] += weight_real * amp_real + weight_imag * amp_imag
                acc_ref[f, 1, rows, :] += weight_real * amp_imag - weight_imag * amp_real
                turned.append(
                    (
                        weight_real * step_cos[member] - weight_imag * step_sin[member],
                        weight_imag * step_cos[member] + weight_real * step_sin[member],
                    )
                )
            return tuple(turned)

        start = tuple((geo_ref[0, rows, :], geo_ref[1, rows, :]) for rows in spans)
        lax.fori_loop(0, freqs, freq_body, start, unroll=freq_unroll)
        return carry

    lax.fori_loop(0, blocks // block_group, block_body, 0)

    @pl.when(pl.program_id(0) == pl.num_programs(0) - 1)
    def _():
        flat = acc_ref[...].reshape(freqs * 2 * observers, lanes)
        out_ref[...] = lax.dot_general(
            jnp.ones((8, lanes), jnp.float32),
            flat,
            (((1,), (1,)), ((), ())),
            precision=lax.Precision.HIGHEST,
            preferred_element_type=jnp.float32,
        )


def field_geometry(panel_position, observer_position, wave_numbers):
    offsets = observer_position[:, :, None] - panel_position[:, None, :]
    distance = jnp.sqrt(offsets[0] * offsets[0] + offsets[1] * offsets[1] + offsets[2] * offsets[2])
    inverse = 1.0 / distance
    first_phase = wave_numbers[0] * distance
    step_phase = wave_step * distance
    return jnp.stack(
        [
            jnp.cos(first_phase) * inverse,
            jnp.sin(first_phase) * inverse,
            jnp.cos(step_phase),
            jnp.sin(step_phase),
            offsets[0] * inverse * inverse,
            offsets[1] * inverse * inverse,
            offsets[2] * inverse * inverse,
            distance,
        ]
    )


def field_chunks(sources, chunk_ids, geometry, wave_numbers):
    rows, columns = sources.shape
    freqs = columns // 8
    observers = geometry.shape[1]
    kernel = functools.partial(field_kernel, math.gcd(observers // 8, 4), 2)
    return pl.pallas_call(
        kernel,
        grid_spec=pltpu.PrefetchScalarGridSpec(
            num_scalar_prefetch=1,
            grid=(rows // 128,),
            in_specs=[
                pl.BlockSpec(memory_space=pltpu.SMEM),
                pl.BlockSpec((8, observers, 128), lambda step, ids: (0, 0, ids[step])),
                pl.BlockSpec((128, columns), lambda step, ids: (step, 0)),
            ],
            out_specs=pl.BlockSpec((8, freqs * 2 * observers), lambda step, ids: (0, 0)),
            scratch_shapes=[
                pltpu.VMEM((freqs, 2, observers, 128), jnp.float32),
                pltpu.VMEM((columns, 128), jnp.float32),
                pltpu.VMEM((columns, 8, 128), jnp.float32),
            ],
        ),
        out_shape=jax.ShapeDtypeStruct((8, freqs * 2 * observers), jnp.float32),
        compiler_params=pltpu.CompilerParams(dimension_semantics=("arbitrary",)),
    )(chunk_ids, wave_numbers, geometry, sources)


def partner_pairs(groups, bit):
    return [(k, k ^ bit) for k in range(groups)]


def quad_pairs(groups, shift):
    low = groups // 4
    return [(k, ((k // low + shift) % 4) * low + k % low) for k in range(groups)]


def halving_sum(blocks, bits):
    groups = blocks.shape[0]
    place = lax.axis_index("obs")
    current = blocks
    for bit in bits:
        split = current.reshape((current.shape[0] // 2, 2) + current.shape[1:])
        mine = (place // bit) % 2
        keep = lax.dynamic_index_in_dim(split, mine, 1, keepdims=False)
        send = lax.dynamic_index_in_dim(split, 1 - mine, 1, keepdims=False)
        current = keep + lax.ppermute(send, "obs", partner_pairs(groups, bit))
    quarter = place // (groups // 4)
    total = lax.dynamic_index_in_dim(current, quarter, 0, keepdims=False)
    for shift in (1, 2, 3):
        piece = lax.dynamic_index_in_dim(current, (quarter + shift) % 4, 0, keepdims=False)
        total = total + lax.ppermute(piece, "obs", quad_pairs(groups, shift))
    return total


def gather_and_sum(own, bits, groups, geometry, wave_numbers):
    place = lax.axis_index("obs")
    columns = own.shape[-1]
    low = groups // 4
    quarter = place // low
    arrived = jnp.stack(
        [own] + [lax.ppermute(own, "obs", quad_pairs(groups, shift)) for shift in (1, 2, 3)]
    )
    known = jnp.stack(
        [lax.dynamic_index_in_dim(arrived, (quarter - k) % 4, 0, keepdims=False) for k in range(4)]
    )[None]
    known_ids = (place % low)[None].astype(jnp.int32)
    partials = [field_chunks(known.reshape(-1, columns), known_ids, geometry, wave_numbers)]
    for turn, bit in enumerate(reversed(bits)):
        other = lax.ppermute(known, "obs", partner_pairs(groups, bit))
        other_ids = jnp.bitwise_xor(known_ids, bit)
        partials.append(field_chunks(other.reshape(-1, columns), other_ids, geometry, wave_numbers))
        if turn + 1 < len(bits):
            known = jnp.concatenate([known, other], axis=0)
            known_ids = jnp.concatenate([known_ids, other_ids], axis=0)
    total = partials[0]
    for part in partials[1:]:
        total = total + part
    return total


def shards(cell_spectra, cell_weight, cell_owner, cell_local, panel_position, observer_position):
    cell_rows, columns = cell_spectra.shape
    freqs_dev = columns // 8
    groups = lax.axis_size("obs")
    panel_total = panel_position.shape[1]
    panels_dev = panel_total // groups
    weighted = (cell_weight[:, None] * cell_spectra.astype(jnp.float32)).astype(jnp.bfloat16)
    panel_number = jnp.arange(panel_total, dtype=jnp.int32)[:, None]
    selector = (
        (panel_number // panels_dev == cell_owner[:, 0][None, :])
        & (panel_number % panels_dev == cell_local[None, :])
    ).astype(jnp.bfloat16)
    local_source = jnp.dot(selector, weighted, preferred_element_type=jnp.float32)
    group_first = lax.axis_index("freq") * freqs_dev
    wave_numbers = wave_step * (
        (group_first + jnp.arange(freqs_dev, dtype=jnp.int32)).astype(jnp.float32) + 1.0
    )
    blocks = local_source.reshape(groups, panels_dev, columns)
    geometry = field_geometry(panel_position, observer_position, wave_numbers)
    observers = observer_position.shape[1]
    if groups & (groups - 1) == 0 and groups >= 16 and 4 * panels_dev == 128:
        bits = [1 << k for k in range(groups.bit_length() - 3)]
        own_source = halving_sum(blocks, bits)
        chunked = jnp.transpose(
            geometry.reshape(8, observers, 4, groups // 4, panels_dev), (0, 1, 3, 2, 4)
        ).reshape(geometry.shape)
        summed = gather_and_sum(own_source, bits, groups, chunked, wave_numbers)
    else:
        own_source = jnp.sum(lax.all_to_all(blocks, "obs", 0, 0, tiled=True), axis=0)
        portion = lax.all_to_all(
            jnp.broadcast_to(own_source[None], blocks.shape), "obs", 0, 0, tiled=True
        ).reshape(panel_total, columns)
        chunk_ids = jnp.arange(panel_total // 128, dtype=jnp.int32)
        summed = field_chunks(portion, chunk_ids, geometry, wave_numbers)
    pressure = summed[0].reshape(freqs_dev, 2, observers) * (reference_radius / math.sqrt(panel_total))
    energy = jnp.sum(pressure[:, 0] * pressure[:, 0] + pressure[:, 1] * pressure[:, 1], axis=0)
    if lax.axis_size("freq") == 2:
        band_total = energy + lax.ppermute(energy, "freq", [(0, 1), (1, 0)])
    else:
        band_total = lax.psum(energy, "freq")
    level = jnp.log(band_total / (freqs_dev * lax.axis_size("freq")) + 1e-06)
    return (pressure, level)


def solution(mesh):
    in_specs = (P("obs", "freq"), P("obs"), P("obs", None), P("obs"), P(), P(None, "obs"))
    out_specs = (P("freq", None, "obs"), P("obs"))
    return jax.shard_map(shards, mesh=mesh, in_specs=in_specs, out_specs=out_specs, check_vma=False)
```

```python
import functools
import math

import jax
import jax.numpy as jnp
from jax import lax
from jax.experimental import pallas as pl
from jax.experimental.pallas import tpu as pltpu
from jax.sharding import PartitionSpec as P

wave_step = 0.1
reference_radius = 10.0


def field_kernel(block_group, freq_unroll, scale, wave_ref, geo_ref, src_ref, out_ref, acc_ref, chan_ref, spread_ref):
    freqs, _, observers, lanes = acc_ref.shape
    blocks = observers // 8
    chunk = pl.program_id(0)

    chan_ref[...] = jnp.transpose(src_ref[...])

    def spread_body(row, carry):
        spread_ref[row] = jnp.broadcast_to(chan_ref[pl.ds(row, 1), :], (8, lanes))
        return carry

    lax.fori_loop(0, chan_ref.shape[0], spread_body, 0, unroll=8)

    def sweep(first):
        def block_body(group, carry):
            spans = [
                pl.ds(pl.multiple_of((group * block_group + member) * 8, 8), 8)
                for member in range(block_group)
            ]
            step_cos = [geo_ref[2, rows, :] for rows in spans]
            step_sin = [geo_ref[3, rows, :] for rows in spans]
            along = [[geo_ref[4 + j, rows, :] for j in range(3)] for rows in spans]
            distance = [geo_ref[7, rows, :] for rows in spans]

            def freq_body(f, phase):
                base = f * 8
                channel = [spread_ref[base + c] for c in range(8)]
                wave = wave_ref[f]
                turned = []
                for member, rows in enumerate(spans):
                    weight_real, weight_imag = phase[member]
                    g = along[member]
                    wave_distance = wave * distance[member]
                    dipole_real = g[0] * channel[2] + g[1] * channel[4] + g[2] * channel[6]
                    dipole_imag = g[0] * channel[3] + g[1] * channel[5] + g[2] * channel[7]
                    amp_real = channel[0] + dipole_real - wave_distance * dipole_imag
                    amp_imag = channel[1] + dipole_imag + wave_distance * dipole_real
                    real_term = weight_real * amp_real + weight_imag * amp_imag
                    imag_term = weight_real * amp_imag - weight_imag * amp_real
                    if first:
                        acc_ref[f, 0, rows, :] = real_term
                        acc_ref[f, 1, rows, :] = imag_term
                    else:
                        acc_ref[f, 0, rows, :] += real_term
                        acc_ref[f, 1, rows, :] += imag_term
                    turned.append(
                        (
                            weight_real * step_cos[member] - weight_imag * step_sin[member],
                            weight_imag * step_cos[member] + weight_real * step_sin[member],
                        )
                    )
                return tuple(turned)

            start = tuple((geo_ref[0, rows, :], geo_ref[1, rows, :]) for rows in spans)
            lax.fori_loop(0, freqs, freq_body, start, unroll=freq_unroll)
            return carry

        lax.fori_loop(0, blocks // block_group, block_body, 0)

    @pl.when(chunk == 0)
    def _():
        sweep(True)

    @pl.when(chunk > 0)
    def _():
        sweep(False)

    @pl.when(chunk == pl.num_programs(0) - 1)
    def _():
        def fold_body(row, carry):
            f = row // 2
            part = row % 2
            flipped = jnp.transpose(acc_ref[f, part])
            out_ref[f, pl.ds(part, 1), :] = jnp.sum(flipped, axis=0, keepdims=True) * scale
            return carry

        lax.fori_loop(0, freqs * 2, fold_body, 0)


def far_field(portion, panel_position, observer_position, wave_numbers, scale):
    panel_total, columns = portion.shape
    freqs = columns // 8
    observers = observer_position.shape[1]
    offsets = observer_position[:, :, None] - panel_position[:, None, :]
    distance = jnp.sqrt(offsets[0] * offsets[0] + offsets[1] * offsets[1] + offsets[2] * offsets[2])
    inverse = 1.0 / distance
    first_phase = wave_numbers[0] * distance
    step_phase = wave_step * distance
    geometry = jnp.stack(
        [
            jnp.cos(first_phase) * inverse,
            jnp.sin(first_phase) * inverse,
            jnp.cos(step_phase),
            jnp.sin(step_phase),
            offsets[0] * inverse * inverse,
            offsets[1] * inverse * inverse,
            offsets[2] * inverse * inverse,
            distance,
        ]
    )
    summed = pl.pallas_call(
        functools.partial(field_kernel, math.gcd(observers // 8, 4), 2, scale),
        grid=(panel_total // 128,),
        in_specs=[
            pl.BlockSpec(memory_space=pltpu.SMEM),
            pl.BlockSpec((8, observers, 128), lambda chunk: (0, 0, chunk)),
            pl.BlockSpec((128, columns), lambda chunk: (chunk, 0)),
        ],
        out_specs=pl.BlockSpec((freqs, 2, observers), lambda chunk: (0, 0, 0)),
        out_shape=jax.ShapeDtypeStruct((freqs, 2, observers), jnp.float32),
        scratch_shapes=[
            pltpu.VMEM((freqs, 2, observers, 128), jnp.float32),
            pltpu.VMEM((columns, 128), jnp.float32),
            pltpu.VMEM((columns, 8, 128), jnp.float32),
        ],
        compiler_params=pltpu.CompilerParams(dimension_semantics=("arbitrary",)),
    )(wave_numbers, geometry, portion)
    return summed


def partner_pairs(groups, bit):
    return [(k, k ^ bit) for k in range(groups)]


def quad_pairs(groups, shift):
    low = groups // 4
    return [(k, ((k // low + shift) % 4) * low + k % low) for k in range(groups)]


def halving_sum(blocks, bits):
    groups = blocks.shape[0]
    place = lax.axis_index("obs")
    current = blocks
    for bit in bits:
        split = current.reshape((current.shape[0] // 2, 2) + current.shape[1:])
        mine = (place // bit) % 2
        keep = lax.dynamic_index_in_dim(split, mine, 1, keepdims=False)
        send = lax.dynamic_index_in_dim(split, 1 - mine, 1, keepdims=False)
        current = keep + lax.ppermute(send, "obs", partner_pairs(groups, bit))
    quarter = place // (groups // 4)
    total = lax.dynamic_index_in_dim(current, quarter, 0, keepdims=False)
    for shift in (1, 2, 3):
        piece = lax.dynamic_index_in_dim(current, (quarter + shift) % 4, 0, keepdims=False)
        total = total + lax.ppermute(piece, "obs", quad_pairs(groups, shift))
    return total


def doubling_gather(own, bits, groups):
    place = lax.axis_index("obs")
    quarter = place // (groups // 4)
    arrived = jnp.stack(
        [own] + [lax.ppermute(own, "obs", quad_pairs(groups, shift)) for shift in (1, 2, 3)]
    )
    gathered = jnp.stack(
        [lax.dynamic_index_in_dim(arrived, (quarter - k) % 4, 0, keepdims=False) for k in range(4)]
    )
    for bit in reversed(bits):
        mine = (place // bit) % 2
        other = lax.ppermute(gathered, "obs", partner_pairs(groups, bit))
        low = jnp.where(mine == 0, gathered, other)
        high = jnp.where(mine == 0, other, gathered)
        gathered = jnp.stack([low, high], axis=1).reshape((-1,) + gathered.shape[1:])
    return gathered


def shards(cell_spectra, cell_weight, cell_owner, cell_local, panel_position, observer_position):
    cell_rows, columns = cell_spectra.shape
    freqs_dev = columns // 8
    groups = lax.axis_size("obs")
    panel_total = panel_position.shape[1]
    panels_dev = panel_total // groups
    weighted = (cell_weight[:, None] * cell_spectra.astype(jnp.float32)).astype(jnp.bfloat16)
    panel_number = jnp.arange(panel_total, dtype=jnp.int32)[:, None]
    selector = (
        (panel_number // panels_dev == cell_owner[:, 0][None, :])
        & (panel_number % panels_dev == cell_local[None, :])
    ).astype(jnp.bfloat16)
    local_source = jnp.dot(selector, weighted, preferred_element_type=jnp.float32)
    group_first = lax.axis_index("freq") * freqs_dev
    wave_numbers = wave_step * (
        (group_first + jnp.arange(freqs_dev, dtype=jnp.int32)).astype(jnp.float32) + 1.0
    )
    blocks = local_source.reshape(groups, panels_dev, columns)
    if groups & (groups - 1) == 0 and groups >= 4:
        bits = [1 << k for k in range(groups.bit_length() - 3)]
        own_source = halving_sum(blocks, bits)
        portion = doubling_gather(own_source, bits, groups).reshape(panel_total, columns)
    else:
        own_source = jnp.sum(lax.all_to_all(blocks, "obs", 0, 0, tiled=True), axis=0)
        portion = lax.all_to_all(
            jnp.broadcast_to(own_source[None], blocks.shape), "obs", 0, 0, tiled=True
        ).reshape(panel_total, columns)
    pressure = far_field(
        portion, panel_position, observer_position, wave_numbers, reference_radius / math.sqrt(panel_total)
    )
    energy = jnp.sum(pressure[:, 0] * pressure[:, 0] + pressure[:, 1] * pressure[:, 1], axis=0)
    if lax.axis_size("freq") == 2:
        band_total = energy + lax.ppermute(energy, "freq", [(0, 1), (1, 0)])
    else:
        band_total = lax.psum(energy, "freq")
    level = jnp.log(band_total / (freqs_dev * lax.axis_size("freq")) + 1e-06)
    return (pressure, level)


def solution(mesh):
    in_specs = (P("obs", "freq"), P("obs"), P("obs", None), P("obs"), P(), P(None, "obs"))
    out_specs = (P("freq", None, "obs"), P("obs"))
    return jax.shard_map(shards, mesh=mesh, in_specs=in_specs, out_specs=out_specs, check_vma=False)
```

```python
import functools
import math

import jax
import jax.numpy as jnp
from jax import lax
from jax.experimental import pallas as pl
from jax.experimental.pallas import tpu as pltpu
from jax.sharding import PartitionSpec as P

wave_step = 0.1
reference_radius = 10.0


def field_kernel(
    block_group, freq_unroll, low_chunks, wave_ref, geo_ref, low_ref, high_ref, out_ref, acc_ref, chan_ref, spread_ref
):
    freqs, _, observers, lanes = acc_ref.shape
    blocks = observers // 8

    @pl.when(pl.program_id(0) == 0)
    def _():
        acc_ref[...] = jnp.zeros(acc_ref.shape, acc_ref.dtype)

    chunk = pl.program_id(0)

    @pl.when(chunk < low_chunks)
    def _():
        chan_ref[...] = jnp.transpose(low_ref[...])

    @pl.when(chunk >= low_chunks)
    def _():
        chan_ref[...] = jnp.transpose(high_ref[...])

    def spread_body(row, carry):
        spread_ref[row] = jnp.broadcast_to(chan_ref[pl.ds(row, 1), :], (8, lanes))
        return carry

    lax.fori_loop(0, chan_ref.shape[0], spread_body, 0, unroll=8)

    def block_body(group, carry):
        spans = [
            pl.ds(pl.multiple_of((group * block_group + member) * 8, 8), 8)
            for member in range(block_group)
        ]
        step_cos = [geo_ref[2, rows, :] for rows in spans]
        step_sin = [geo_ref[3, rows, :] for rows in spans]
        along = [[geo_ref[4 + j, rows, :] for j in range(3)] for rows in spans]
        distance = [geo_ref[7, rows, :] for rows in spans]

        def freq_body(f, phase):
            base = f * 8
            channel = [spread_ref[base + c] for c in range(8)]
            wave = wave_ref[f]
            turned = []
            for member, rows in enumerate(spans):
                weight_real, weight_imag = phase[member]
                g = along[member]
                wave_distance = wave * distance[member]
                dipole_real = g[0] * channel[2] + g[1] * channel[4] + g[2] * channel[6]
                dipole_imag = g[0] * channel[3] + g[1] * channel[5] + g[2] * channel[7]
                amp_real = channel[0] + dipole_real - wave_distance * dipole_imag
                amp_imag = channel[1] + dipole_imag + wave_distance * dipole_real
                acc_ref[f, 0, rows, :] += weight_real * amp_real + weight_imag * amp_imag
                acc_ref[f, 1, rows, :] += weight_real * amp_imag - weight_imag * amp_real
                turned.append(
                    (
                        weight_real * step_cos[member] - weight_imag * step_sin[member],
                        weight_imag * step_cos[member] + weight_real * step_sin[member],
                    )
                )
            return tuple(turned)

        start = tuple((geo_ref[0, rows, :], geo_ref[1, rows, :]) for rows in spans)
        lax.fori_loop(0, freqs, freq_body, start, unroll=freq_unroll)
        return carry

    lax.fori_loop(0, blocks // block_group, block_body, 0)

    @pl.when(pl.program_id(0) == pl.num_programs(0) - 1)
    def _():
        flat = acc_ref[...].reshape(freqs * 2 * observers, lanes)
        out_ref[...] = lax.dot_general(
            jnp.ones((8, lanes), jnp.float32),
            flat,
            (((1,), (1,)), ((), ())),
            precision=lax.Precision.HIGHEST,
            preferred_element_type=jnp.float32,
        )


def far_field(low, high, panel_position, observer_position, wave_numbers):
    columns = low.shape[1]
    low_chunks = low.shape[0] // 128
    panel_total = low.shape[0] + high.shape[0]
    freqs = columns // 8
    observers = observer_position.shape[1]
    offsets = observer_position[:, :, None] - panel_position[:, None, :]
    distance = jnp.sqrt(offsets[0] * offsets[0] + offsets[1] * offsets[1] + offsets[2] * offsets[2])
    inverse = 1.0 / distance
    first_phase = wave_numbers[0] * distance
    step_phase = wave_step * distance
    geometry = jnp.stack(
        [
            jnp.cos(first_phase) * inverse,
            jnp.sin(first_phase) * inverse,
            jnp.cos(step_phase),
            jnp.sin(step_phase),
            offsets[0] * inverse * inverse,
            offsets[1] * inverse * inverse,
            offsets[2] * inverse * inverse,
            distance,
        ]
    )
    summed = pl.pallas_call(
        functools.partial(field_kernel, math.gcd(observers // 8, 4), 2, low_chunks),
        grid=(panel_total // 128,),
        in_specs=[
            pl.BlockSpec(memory_space=pltpu.SMEM),
            pl.BlockSpec((8, observers, 128), lambda chunk: (0, 0, chunk)),
            pl.BlockSpec((128, columns), lambda chunk: (jnp.minimum(chunk, low_chunks - 1), 0)),
            pl.BlockSpec((128, columns), lambda chunk: (jnp.maximum(chunk - low_chunks, 0), 0)),
        ],
        out_specs=pl.BlockSpec((8, freqs * 2 * observers), lambda chunk: (0, 0)),
        out_shape=jax.ShapeDtypeStruct((8, freqs * 2 * observers), jnp.float32),
        scratch_shapes=[
            pltpu.VMEM((freqs, 2, observers, 128), jnp.float32),
            pltpu.VMEM((columns, 128), jnp.float32),
            pltpu.VMEM((columns, 8, 128), jnp.float32),
        ],
        compiler_params=pltpu.CompilerParams(dimension_semantics=("arbitrary",)),
    )(wave_numbers, geometry, low, high)
    return summed[0].reshape(freqs, 2, observers)


def partner_pairs(groups, bit):
    return [(k, k ^ bit) for k in range(groups)]


def quad_pairs(groups, shift):
    low = groups // 4
    return [(k, ((k // low + shift) % 4) * low + k % low) for k in range(groups)]


def halving_sum(blocks, bits):
    groups = blocks.shape[0]
    place = lax.axis_index("obs")
    current = blocks
    for bit in bits:
        split = current.reshape((current.shape[0] // 2, 2) + current.shape[1:])
        mine = (place // bit) % 2
        keep = lax.dynamic_index_in_dim(split, mine, 1, keepdims=False)
        send = lax.dynamic_index_in_dim(split, 1 - mine, 1, keepdims=False)
        current = keep + lax.ppermute(send, "obs", partner_pairs(groups, bit))
    quarter = place // (groups // 4)
    total = lax.dynamic_index_in_dim(current, quarter, 0, keepdims=False)
    for shift in (1, 2, 3):
        piece = lax.dynamic_index_in_dim(current, (quarter + shift) % 4, 0, keepdims=False)
        total = total + lax.ppermute(piece, "obs", quad_pairs(groups, shift))
    return total


def doubling_gather(own, bits, groups):
    place = lax.axis_index("obs")
    quarter = place // (groups // 4)
    arrived = jnp.stack(
        [own] + [lax.ppermute(own, "obs", quad_pairs(groups, shift)) for shift in (1, 2, 3)]
    )
    gathered = jnp.stack(
        [lax.dynamic_index_in_dim(arrived, (quarter - k) % 4, 0, keepdims=False) for k in range(4)]
    )
    for bit in reversed(bits):
        mine = (place // bit) % 2
        other = lax.ppermute(gathered, "obs", partner_pairs(groups, bit))
        if bit == 1:
            return gathered, other
        low = jnp.where(mine == 0, gathered, other)
        high = jnp.where(mine == 0, other, gathered)
        gathered = jnp.stack([low, high], axis=1).reshape((-1,) + gathered.shape[1:])
    return gathered


def shards(cell_spectra, cell_weight, cell_owner, cell_local, panel_position, observer_position):
    cell_rows, columns = cell_spectra.shape
    freqs_dev = columns // 8
    groups = lax.axis_size("obs")
    panel_total = panel_position.shape[1]
    panels_dev = panel_total // groups
    weighted = (cell_weight[:, None] * cell_spectra.astype(jnp.float32)).astype(jnp.bfloat16)
    panel_number = jnp.arange(panel_total, dtype=jnp.int32)[:, None]
    selector = (
        (panel_number // panels_dev == cell_owner[:, 0][None, :])
        & (panel_number % panels_dev == cell_local[None, :])
    ).astype(jnp.bfloat16)
    local_source = jnp.dot(selector, weighted, preferred_element_type=jnp.float32)
    group_first = lax.axis_index("freq") * freqs_dev
    wave_numbers = wave_step * (
        (group_first + jnp.arange(freqs_dev, dtype=jnp.int32)).astype(jnp.float32) + 1.0
    )
    blocks = local_source.reshape(groups, panels_dev, columns)
    if groups & (groups - 1) == 0 and groups >= 8:
        bits = [1 << k for k in range(groups.bit_length() - 3)]
        own_source = halving_sum(blocks, bits)
        mine_half, other_half = doubling_gather(own_source, bits, groups)
        mine = lax.axis_index("obs") % 2
        paired = panel_position.reshape(3, groups // 2, 2, panels_dev)
        ordered = jnp.concatenate(
            [
                lax.dynamic_index_in_dim(paired, mine, 2, keepdims=False),
                lax.dynamic_index_in_dim(paired, 1 - mine, 2, keepdims=False),
            ],
            axis=1,
        ).reshape(3, panel_total)
        summed = far_field(
            mine_half.reshape(-1, columns),
            other_half.reshape(-1, columns),
            ordered,
            observer_position,
            wave_numbers,
        )
    else:
        own_source = jnp.sum(lax.all_to_all(blocks, "obs", 0, 0, tiled=True), axis=0)
        portion = lax.all_to_all(
            jnp.broadcast_to(own_source[None], blocks.shape), "obs", 0, 0, tiled=True
        ).reshape(panel_total, columns)
        half = panel_total // 256 * 128
        summed = far_field(portion[:half], portion[half:], panel_position, observer_position, wave_numbers)
    pressure = summed * (reference_radius / math.sqrt(panel_total))
    energy = jnp.sum(pressure[:, 0] * pressure[:, 0] + pressure[:, 1] * pressure[:, 1], axis=0)
    if lax.axis_size("freq") == 2:
        band_total = energy + lax.ppermute(energy, "freq", [(0, 1), (1, 0)])
    else:
        band_total = lax.psum(energy, "freq")
    level = jnp.log(band_total / (freqs_dev * lax.axis_size("freq")) + 1e-06)
    return (pressure, level)


def solution(mesh):
    in_specs = (P("obs", "freq"), P("obs"), P("obs", None), P("obs"), P(), P(None, "obs"))
    out_specs = (P("freq", None, "obs"), P("obs"))
    return jax.shard_map(shards, mesh=mesh, in_specs=in_specs, out_specs=out_specs, check_vma=False)
```

```python
import functools
import math

import jax
import jax.numpy as jnp
from jax import lax
from jax.experimental import pallas as pl
from jax.experimental.pallas import tpu as pltpu
from jax.sharding import PartitionSpec as P

wave_step = 0.1
reference_radius = 10.0


def field_kernel(block_group, freq_unroll, wave_ref, geo_ref, src_ref, out_ref, acc_ref, chan_ref, spread_ref):
    freqs, _, observers, lanes = acc_ref.shape
    blocks = observers // 8

    @pl.when(pl.program_id(0) == 0)
    def _():
        acc_ref[...] = jnp.zeros(acc_ref.shape, acc_ref.dtype)

    chan_ref[...] = jnp.transpose(src_ref[...])

    def spread_body(row, carry):
        spread_ref[row] = jnp.broadcast_to(chan_ref[pl.ds(row, 1), :], (8, lanes))
        return carry

    lax.fori_loop(0, chan_ref.shape[0], spread_body, 0, unroll=8)

    def block_body(group, carry):
        spans = [
            pl.ds(pl.multiple_of((group * block_group + member) * 8, 8), 8)
            for member in range(block_group)
        ]
        step_cos = [geo_ref[2, rows, :] for rows in spans]
        step_sin = [geo_ref[3, rows, :] for rows in spans]
        along = [[geo_ref[4 + j, rows, :] for j in range(3)] for rows in spans]
        distance = [geo_ref[7, rows, :] for rows in spans]

        def freq_body(f, phase):
            base = f * 8
            channel = [spread_ref[base + c] for c in range(8)]
            wave = wave_ref[f]
            turned = []
            for member, rows in enumerate(spans):
                weight_real, weight_imag = phase[member]
                g = along[member]
                wave_distance = wave * distance[member]
                dipole_real = g[0] * channel[2] + g[1] * channel[4] + g[2] * channel[6]
                dipole_imag = g[0] * channel[3] + g[1] * channel[5] + g[2] * channel[7]
                amp_real = channel[0] + dipole_real - wave_distance * dipole_imag
                amp_imag = channel[1] + dipole_imag + wave_distance * dipole_real
                acc_ref[f, 0, rows, :] += weight_real * amp_real + weight_imag * amp_imag
                acc_ref[f, 1, rows, :] += weight_real * amp_imag - weight_imag * amp_real
                turned.append(
                    (
                        weight_real * step_cos[member] - weight_imag * step_sin[member],
                        weight_imag * step_cos[member] + weight_real * step_sin[member],
                    )
                )
            return tuple(turned)

        start = tuple((geo_ref[0, rows, :], geo_ref[1, rows, :]) for rows in spans)
        lax.fori_loop(0, freqs, freq_body, start, unroll=freq_unroll)
        return carry

    lax.fori_loop(0, blocks // block_group, block_body, 0)

    @pl.when(pl.program_id(0) == pl.num_programs(0) - 1)
    def _():
        flat = acc_ref[...].reshape(freqs * 2 * observers, lanes)
        out_ref[...] = lax.dot_general(
            jnp.ones((8, lanes), jnp.float32),
            flat,
            (((1,), (1,)), ((), ())),
            precision=lax.Precision.HIGHEST,
            preferred_element_type=jnp.float32,
        )


def far_field(portion, panel_position, observer_position, wave_numbers):
    panel_total, columns = portion.shape
    freqs = columns // 8
    observers = observer_position.shape[1]
    offsets = observer_position[:, :, None] - panel_position[:, None, :]
    distance = jnp.sqrt(offsets[0] * offsets[0] + offsets[1] * offsets[1] + offsets[2] * offsets[2])
    inverse = 1.0 / distance
    first_phase = wave_numbers[0] * distance
    step_phase = wave_step * distance
    geometry = jnp.stack(
        [
            jnp.cos(first_phase) * inverse,
            jnp.sin(first_phase) * inverse,
            jnp.cos(step_phase),
            jnp.sin(step_phase),
            offsets[0] * inverse * inverse,
            offsets[1] * inverse * inverse,
            offsets[2] * inverse * inverse,
            distance,
        ]
    )
    summed = pl.pallas_call(
        functools.partial(field_kernel, math.gcd(observers // 8, 4), 2),
        grid=(panel_total // 128,),
        in_specs=[
            pl.BlockSpec(memory_space=pltpu.SMEM),
            pl.BlockSpec((8, observers, 128), lambda chunk: (0, 0, chunk)),
            pl.BlockSpec((128, columns), lambda chunk: (chunk, 0)),
        ],
        out_specs=pl.BlockSpec((8, freqs * 2 * observers), lambda chunk: (0, 0)),
        out_shape=jax.ShapeDtypeStruct((8, freqs * 2 * observers), jnp.float32),
        scratch_shapes=[
            pltpu.VMEM((freqs, 2, observers, 128), jnp.float32),
            pltpu.VMEM((columns, 128), jnp.float32),
            pltpu.VMEM((columns, 8, 128), jnp.float32),
        ],
        compiler_params=pltpu.CompilerParams(dimension_semantics=("arbitrary",)),
    )(wave_numbers, geometry, portion)
    return summed[0].reshape(freqs, 2, observers)


def partner_pairs(groups, bit):
    return [(k, k ^ bit) for k in range(groups)]


def quad_pairs(groups, shift):
    low = groups // 4
    return [(k, ((k // low + shift) % 4) * low + k % low) for k in range(groups)]


def halving_sum(keep_first, send_first, bits, groups):
    place = lax.axis_index("obs")
    current = keep_first + lax.ppermute(send_first, "obs", partner_pairs(groups, bits[0]))
    for bit in bits[1:]:
        split = current.reshape((current.shape[0] // 2, 2) + current.shape[1:])
        mine = (place // bit) % 2
        keep = lax.dynamic_index_in_dim(split, mine, 1, keepdims=False)
        send = lax.dynamic_index_in_dim(split, 1 - mine, 1, keepdims=False)
        current = keep + lax.ppermute(send, "obs", partner_pairs(groups, bit))
    quarter = place // (groups // 4)
    total = lax.dynamic_index_in_dim(current, quarter, 0, keepdims=False)
    for shift in (1, 2, 3):
        piece = lax.dynamic_index_in_dim(current, (quarter + shift) % 4, 0, keepdims=False)
        total = total + lax.ppermute(piece, "obs", quad_pairs(groups, shift))
    return total


def doubling_gather(own, bits, groups):
    place = lax.axis_index("obs")
    quarter = place // (groups // 4)
    arrived = jnp.stack(
        [own] + [lax.ppermute(own, "obs", quad_pairs(groups, shift)) for shift in (1, 2, 3)]
    )
    gathered = jnp.stack(
        [lax.dynamic_index_in_dim(arrived, (quarter - k) % 4, 0, keepdims=False) for k in range(4)]
    )
    for bit in reversed(bits):
        mine = (place // bit) % 2
        other = lax.ppermute(gathered, "obs", partner_pairs(groups, bit))
        low = jnp.where(mine == 0, gathered, other)
        high = jnp.where(mine == 0, other, gathered)
        gathered = jnp.stack([low, high], axis=1).reshape((-1,) + gathered.shape[1:])
    return gathered


def shards(cell_spectra, cell_weight, cell_owner, cell_local, panel_position, observer_position):
    cell_rows, columns = cell_spectra.shape
    freqs_dev = columns // 8
    groups = lax.axis_size("obs")
    panel_total = panel_position.shape[1]
    panels_dev = panel_total // groups
    weighted = (cell_weight[:, None] * cell_spectra.astype(jnp.float32)).astype(jnp.bfloat16)
    owners = cell_owner[:, 0][None, :]
    slots = cell_local[None, :]
    group_first = lax.axis_index("freq") * freqs_dev
    wave_numbers = wave_step * (
        (group_first + jnp.arange(freqs_dev, dtype=jnp.int32)).astype(jnp.float32) + 1.0
    )

    def source_of(panel_number):
        selector = (
            (panel_number // panels_dev == owners) & (panel_number % panels_dev == slots)
        ).astype(jnp.bfloat16)
        return jnp.dot(selector, weighted, preferred_element_type=jnp.float32)

    if groups & (groups - 1) == 0 and groups >= 8:
        bits = [1 << k for k in range(groups.bit_length() - 3)]
        mine = lax.axis_index("obs") % 2

        def half_panels(parity):
            pair = 2 * jnp.arange(groups // 2, dtype=jnp.int32)[:, None] + parity
            return (pair * panels_dev + jnp.arange(panels_dev, dtype=jnp.int32)[None, :]).reshape(-1, 1)

        send_first = source_of(half_panels(1 - mine)).reshape(groups // 2, panels_dev, columns)
        keep_first = source_of(half_panels(mine)).reshape(groups // 2, panels_dev, columns)
        own_source = halving_sum(keep_first, send_first, bits, groups)
        portion = doubling_gather(own_source, bits, groups).reshape(panel_total, columns)
    else:
        blocks = source_of(jnp.arange(panel_total, dtype=jnp.int32)[:, None]).reshape(
            groups, panels_dev, columns
        )
        own_source = jnp.sum(lax.all_to_all(blocks, "obs", 0, 0, tiled=True), axis=0)
        portion = lax.all_to_all(
            jnp.broadcast_to(own_source[None], blocks.shape), "obs", 0, 0, tiled=True
        ).reshape(panel_total, columns)
    summed = far_field(portion, panel_position, observer_position, wave_numbers)
    pressure = summed * (reference_radius / math.sqrt(panel_total))
    energy = jnp.sum(pressure[:, 0] * pressure[:, 0] + pressure[:, 1] * pressure[:, 1], axis=0)
    if lax.axis_size("freq") == 2:
        band_total = energy + lax.ppermute(energy, "freq", [(0, 1), (1, 0)])
    else:
        band_total = lax.psum(energy, "freq")
    level = jnp.log(band_total / (freqs_dev * lax.axis_size("freq")) + 1e-06)
    return (pressure, level)


def solution(mesh):
    in_specs = (P("obs", "freq"), P("obs"), P("obs", None), P("obs"), P(), P(None, "obs"))
    out_specs = (P("freq", None, "obs"), P("obs"))
    return jax.shard_map(shards, mesh=mesh, in_specs=in_specs, out_specs=out_specs, check_vma=False)
```

```python
import functools
import math

import jax
import jax.numpy as jnp
from jax import lax
from jax.experimental import pallas as pl
from jax.experimental.pallas import tpu as pltpu
from jax.sharding import PartitionSpec as P

wave_step = 0.1
reference_radius = 10.0


def field_kernel(block_group, freq_unroll, wave_ref, geo_ref, src_ref, out_ref, acc_ref, chan_ref, spread_ref):
    freqs, _, observers, lanes = acc_ref.shape
    blocks = observers // 8

    @pl.when(pl.program_id(0) == 0)
    def _():
        acc_ref[...] = jnp.zeros(acc_ref.shape, acc_ref.dtype)

    chan_ref[...] = jnp.transpose(src_ref[...])

    def spread_body(row, carry):
        spread_ref[row] = jnp.broadcast_to(chan_ref[pl.ds(row, 1), :], (8, lanes))
        return carry

    lax.fori_loop(0, chan_ref.shape[0], spread_body, 0, unroll=8)

    def block_body(group, carry):
        spans = [
            pl.ds(pl.multiple_of((group * block_group + member) * 8, 8), 8)
            for member in range(block_group)
        ]
        step_cos = [geo_ref[2, rows, :] for rows in spans]
        step_sin = [geo_ref[3, rows, :] for rows in spans]
        along = [[geo_ref[4 + j, rows, :] for j in range(3)] for rows in spans]
        distance = [geo_ref[7, rows, :] for rows in spans]

        def freq_body(f, phase):
            base = f * 8
            channel = [spread_ref[base + c] for c in range(8)]
            wave = wave_ref[f]
            turned = []
            for member, rows in enumerate(spans):
                weight_real, weight_imag = phase[member]
                g = along[member]
                wave_distance = wave * distance[member]
                dipole_real = g[0] * channel[2] + g[1] * channel[4] + g[2] * channel[6]
                dipole_imag = g[0] * channel[3] + g[1] * channel[5] + g[2] * channel[7]
                amp_real = channel[0] + dipole_real - wave_distance * dipole_imag
                amp_imag = channel[1] + dipole_imag + wave_distance * dipole_real
                acc_ref[f, 0, rows, :] += weight_real * amp_real + weight_imag * amp_imag
                acc_ref[f, 1, rows, :] += weight_real * amp_imag - weight_imag * amp_real
                turned.append(
                    (
                        weight_real * step_cos[member] - weight_imag * step_sin[member],
                        weight_imag * step_cos[member] + weight_real * step_sin[member],
                    )
                )
            return tuple(turned)

        start = tuple((geo_ref[0, rows, :], geo_ref[1, rows, :]) for rows in spans)
        lax.fori_loop(0, freqs, freq_body, start, unroll=freq_unroll)
        return carry

    lax.fori_loop(0, blocks // block_group, block_body, 0)

    @pl.when(pl.program_id(0) == pl.num_programs(0) - 1)
    def _():
        flat = acc_ref[...].reshape(freqs * 2 * observers, lanes)
        spread = lax.broadcasted_iota(jnp.int32, (8, lanes), 1) // (lanes // 8)
        rows = lax.broadcasted_iota(jnp.int32, (8, lanes), 0)
        out_ref[...] = lax.dot_general(
            (spread == rows).astype(jnp.float32),
            flat,
            (((1,), (1,)), ((), ())),
            precision=lax.Precision.HIGHEST,
            preferred_element_type=jnp.float32,
        )


def far_field(portion, panel_position, observer_position, wave_numbers):
    panel_total, columns = portion.shape
    freqs = columns // 8
    observers = observer_position.shape[1]
    offsets = observer_position[:, :, None] - panel_position[:, None, :]
    distance = jnp.sqrt(offsets[0] * offsets[0] + offsets[1] * offsets[1] + offsets[2] * offsets[2])
    inverse = 1.0 / distance
    first_phase = wave_numbers[0] * distance
    step_phase = wave_step * distance
    geometry = jnp.stack(
        [
            jnp.cos(first_phase) * inverse,
            jnp.sin(first_phase) * inverse,
            jnp.cos(step_phase),
            jnp.sin(step_phase),
            offsets[0] * inverse * inverse,
            offsets[1] * inverse * inverse,
            offsets[2] * inverse * inverse,
            distance,
        ]
    )
    summed = pl.pallas_call(
        functools.partial(field_kernel, math.gcd(observers // 8, 4), 2),
        grid=(panel_total // 128,),
        in_specs=[
            pl.BlockSpec(memory_space=pltpu.SMEM),
            pl.BlockSpec((8, observers, 128), lambda chunk: (0, 0, chunk)),
            pl.BlockSpec((128, columns), lambda chunk: (chunk, 0)),
        ],
        out_specs=pl.BlockSpec((8, freqs * 2 * observers), lambda chunk: (0, 0)),
        out_shape=jax.ShapeDtypeStruct((8, freqs * 2 * observers), jnp.float32),
        scratch_shapes=[
            pltpu.VMEM((freqs, 2, observers, 128), jnp.float32),
            pltpu.VMEM((columns, 128), jnp.float32),
            pltpu.VMEM((columns, 8, 128), jnp.float32),
        ],
        compiler_params=pltpu.CompilerParams(dimension_semantics=("arbitrary",)),
    )(wave_numbers, geometry, portion)
    return jnp.sum(summed, axis=0).reshape(freqs, 2, observers)


def partner_pairs(groups, bit):
    return [(k, k ^ bit) for k in range(groups)]


def quad_pairs(groups, shift):
    low = groups // 4
    return [(k, ((k // low + shift) % 4) * low + k % low) for k in range(groups)]


def halving_sum(blocks, bits):
    groups = blocks.shape[0]
    place = lax.axis_index("obs")
    current = blocks
    for bit in bits:
        split = current.reshape((current.shape[0] // 2, 2) + current.shape[1:])
        mine = (place // bit) % 2
        keep = lax.dynamic_index_in_dim(split, mine, 1, keepdims=False)
        send = lax.dynamic_index_in_dim(split, 1 - mine, 1, keepdims=False)
        current = keep + lax.ppermute(send, "obs", partner_pairs(groups, bit))
    quarter = place // (groups // 4)
    total = lax.dynamic_index_in_dim(current, quarter, 0, keepdims=False)
    for shift in (1, 2, 3):
        piece = lax.dynamic_index_in_dim(current, (quarter + shift) % 4, 0, keepdims=False)
        total = total + lax.ppermute(piece, "obs", quad_pairs(groups, shift))
    return total


def doubling_gather(own, bits, groups):
    place = lax.axis_index("obs")
    quarter = place // (groups // 4)
    arrived = jnp.stack(
        [own] + [lax.ppermute(own, "obs", quad_pairs(groups, shift)) for shift in (1, 2, 3)]
    )
    gathered = jnp.stack(
        [lax.dynamic_index_in_dim(arrived, (quarter - k) % 4, 0, keepdims=False) for k in range(4)]
    )
    for bit in reversed(bits):
        mine = (place // bit) % 2
        other = lax.ppermute(gathered, "obs", partner_pairs(groups, bit))
        low = jnp.where(mine == 0, gathered, other)
        high = jnp.where(mine == 0, other, gathered)
        gathered = jnp.stack([low, high], axis=1).reshape((-1,) + gathered.shape[1:])
    return gathered


def shards(cell_spectra, cell_weight, cell_owner, cell_local, panel_position, observer_position):
    cell_rows, columns = cell_spectra.shape
    freqs_dev = columns // 8
    groups = lax.axis_size("obs")
    panel_total = panel_position.shape[1]
    panels_dev = panel_total // groups
    weighted = (cell_weight[:, None] * cell_spectra.astype(jnp.float32)).astype(jnp.bfloat16)
    panel_number = jnp.arange(panel_total, dtype=jnp.int32)[:, None]
    selector = (
        (panel_number // panels_dev == cell_owner[:, 0][None, :])
        & (panel_number % panels_dev == cell_local[None, :])
    ).astype(jnp.bfloat16)
    local_source = jnp.dot(selector, weighted, preferred_element_type=jnp.float32)
    group_first = lax.axis_index("freq") * freqs_dev
    wave_numbers = wave_step * (
        (group_first + jnp.arange(freqs_dev, dtype=jnp.int32)).astype(jnp.float32) + 1.0
    )
    blocks = local_source.reshape(groups, panels_dev, columns)
    if groups & (groups - 1) == 0 and groups >= 4:
        bits = [1 << k for k in range(groups.bit_length() - 3)]
        own_source = halving_sum(blocks, bits)
        portion = doubling_gather(own_source, bits, groups).reshape(panel_total, columns)
    else:
        own_source = jnp.sum(lax.all_to_all(blocks, "obs", 0, 0, tiled=True), axis=0)
        portion = lax.all_to_all(
            jnp.broadcast_to(own_source[None], blocks.shape), "obs", 0, 0, tiled=True
        ).reshape(panel_total, columns)
    summed = far_field(portion, panel_position, observer_position, wave_numbers)
    pressure = summed * (reference_radius / math.sqrt(panel_total))
    energy = jnp.sum(pressure[:, 0] * pressure[:, 0] + pressure[:, 1] * pressure[:, 1], axis=0)
    if lax.axis_size("freq") == 2:
        band_total = energy + lax.ppermute(energy, "freq", [(0, 1), (1, 0)])
    else:
        band_total = lax.psum(energy, "freq")
    level = jnp.log(band_total / (freqs_dev * lax.axis_size("freq")) + 1e-06)
    return (pressure, level)


def solution(mesh):
    in_specs = (P("obs", "freq"), P("obs"), P("obs", None), P("obs"), P(), P(None, "obs"))
    out_specs = (P("freq", None, "obs"), P("obs"))
    return jax.shard_map(shards, mesh=mesh, in_specs=in_specs, out_specs=out_specs, check_vma=False)
```

```python
import functools
import math

import jax
import jax.numpy as jnp
from jax import lax
from jax.experimental import pallas as pl
from jax.experimental.pallas import tpu as pltpu
from jax.sharding import PartitionSpec as P

wave_step = 0.1
reference_radius = 10.0


def field_kernel(block_group, freq_unroll, wave_ref, geo_ref, src_ref, out_ref, acc_ref, chan_ref, spread_ref):
    freqs, _, observers, lanes = acc_ref.shape
    blocks = observers // 8

    @pl.when(pl.program_id(0) == 0)
    def _():
        acc_ref[...] = jnp.zeros(acc_ref.shape, acc_ref.dtype)

    chan_ref[...] = jnp.transpose(src_ref[...])

    def spread_body(row, carry):
        spread_ref[row] = jnp.broadcast_to(chan_ref[pl.ds(row, 1), :], (8, lanes))
        return carry

    lax.fori_loop(0, chan_ref.shape[0], spread_body, 0, unroll=8)

    def block_body(group, carry):
        spans = [
            pl.ds(pl.multiple_of((group * block_group + member) * 8, 8), 8)
            for member in range(block_group)
        ]
        step_cos = [geo_ref[2, rows, :] for rows in spans]
        step_sin = [geo_ref[3, rows, :] for rows in spans]
        along = [[geo_ref[4 + j, rows, :] for j in range(3)] for rows in spans]
        distance = [geo_ref[7, rows, :] for rows in spans]

        def freq_body(f, phase):
            base = f * 8
            channel = [spread_ref[base + c] for c in range(8)]
            wave = wave_ref[f]
            turned = []
            for member, rows in enumerate(spans):
                weight_real, weight_imag = phase[member]
                g = along[member]
                wave_distance = wave * distance[member]
                dipole_real = g[0] * channel[2] + g[1] * channel[4] + g[2] * channel[6]
                dipole_imag = g[0] * channel[3] + g[1] * channel[5] + g[2] * channel[7]
                amp_real = channel[0] + dipole_real - wave_distance * dipole_imag
                amp_imag = channel[1] + dipole_imag + wave_distance * dipole_real
                acc_ref[f, 0, rows, :] += weight_real * amp_real + weight_imag * amp_imag
                acc_ref[f, 1, rows, :] += weight_real * amp_imag - weight_imag * amp_real
                turned.append(
                    (
                        weight_real * step_cos[member] - weight_imag * step_sin[member],
                        weight_imag * step_cos[member] + weight_real * step_sin[member],
                    )
                )
            return tuple(turned)

        start = tuple((geo_ref[0, rows, :], geo_ref[1, rows, :]) for rows in spans)
        lax.fori_loop(0, freqs, freq_body, start, unroll=freq_unroll)
        return carry

    lax.fori_loop(0, blocks // block_group, block_body, 0)

    @pl.when(pl.program_id(0) == pl.num_programs(0) - 1)
    def _():
        flat = acc_ref[...].reshape(freqs * 2 * observers, lanes)
        out_ref[...] = lax.dot_general(
            jnp.ones((8, lanes), jnp.float32),
            flat,
            (((1,), (1,)), ((), ())),
            precision=lax.Precision.HIGHEST,
            preferred_element_type=jnp.float32,
        )


def far_field(portion, panel_position, observer_position, wave_numbers):
    panel_total, columns = portion.shape
    freqs = columns // 8
    observers = observer_position.shape[1]
    offsets = observer_position[:, :, None] - panel_position[:, None, :]
    distance = jnp.sqrt(offsets[0] * offsets[0] + offsets[1] * offsets[1] + offsets[2] * offsets[2])
    inverse = 1.0 / distance
    first_phase = wave_numbers[0] * distance
    step_phase = wave_step * distance
    geometry = jnp.stack(
        [
            jnp.cos(first_phase) * inverse,
            jnp.sin(first_phase) * inverse,
            jnp.cos(step_phase),
            jnp.sin(step_phase),
            offsets[0] * inverse * inverse,
            offsets[1] * inverse * inverse,
            offsets[2] * inverse * inverse,
            distance,
        ]
    )
    summed = pl.pallas_call(
        functools.partial(field_kernel, math.gcd(observers // 8, 4), 2),
        grid=(panel_total // 128,),
        in_specs=[
            pl.BlockSpec(memory_space=pltpu.SMEM),
            pl.BlockSpec((8, observers, 128), lambda chunk: (0, 0, chunk)),
            pl.BlockSpec((128, columns), lambda chunk: (chunk, 0)),
        ],
        out_specs=pl.BlockSpec((8, freqs * 2 * observers), lambda chunk: (0, 0)),
        out_shape=jax.ShapeDtypeStruct((8, freqs * 2 * observers), jnp.float32),
        scratch_shapes=[
            pltpu.VMEM((freqs, 2, observers, 128), jnp.float32),
            pltpu.VMEM((columns, 128), jnp.float32),
            pltpu.VMEM((columns, 8, 128), jnp.float32),
        ],
        compiler_params=pltpu.CompilerParams(dimension_semantics=("arbitrary",)),
    )(wave_numbers, geometry, portion)
    return summed[0].reshape(freqs, 2, observers)


def partner_pairs(groups, bit):
    return [(k, k ^ bit) for k in range(groups)]


def quad_pairs(groups, shift):
    low = groups // 4
    return [(k, ((k // low + shift) % 4) * low + k % low) for k in range(groups)]


def halving_sum(blocks, bits):
    groups = blocks.shape[0]
    place = lax.axis_index("obs")
    current = blocks
    for bit in bits:
        split = current.reshape((current.shape[0] // 2, 2) + current.shape[1:])
        mine = (place // bit) % 2
        keep = lax.dynamic_index_in_dim(split, mine, 1, keepdims=False)
        send = lax.dynamic_index_in_dim(split, 1 - mine, 1, keepdims=False)
        current = keep + lax.ppermute(send, "obs", partner_pairs(groups, bit))
    quarter = place // (groups // 4)
    total = lax.dynamic_index_in_dim(current, quarter, 0, keepdims=False)
    for shift in (1, 2, 3):
        piece = lax.dynamic_index_in_dim(current, (quarter + shift) % 4, 0, keepdims=False)
        total = total + lax.ppermute(piece, "obs", quad_pairs(groups, shift))
    return total


def doubling_gather(own, bits, groups):
    place = lax.axis_index("obs")
    quarter = place // (groups // 4)
    arrived = jnp.stack(
        [own] + [lax.ppermute(own, "obs", quad_pairs(groups, shift)) for shift in (1, 2, 3)]
    )
    gathered = jnp.stack(
        [lax.dynamic_index_in_dim(arrived, (quarter - k) % 4, 0, keepdims=False) for k in range(4)]
    )
    for bit in reversed(bits):
        mine = (place // bit) % 2
        other = lax.ppermute(gathered, "obs", partner_pairs(groups, bit))
        low = jnp.where(mine == 0, gathered, other)
        high = jnp.where(mine == 0, other, gathered)
        gathered = jnp.stack([low, high], axis=1).reshape((-1,) + gathered.shape[1:])
    return gathered


def shards(cell_spectra, cell_weight, cell_owner, cell_local, panel_position, observer_position):
    cell_rows, columns = cell_spectra.shape
    freqs_dev = columns // 8
    groups = lax.axis_size("obs")
    panel_total = panel_position.shape[1]
    panels_dev = panel_total // groups
    weighted = (cell_weight[:, None] * cell_spectra.astype(jnp.float32)).astype(jnp.bfloat16)
    panel_number = jnp.arange(panel_total, dtype=jnp.int32)[:, None]
    selector = (
        (panel_number // panels_dev == cell_owner[:, 0][None, :])
        & (panel_number % panels_dev == cell_local[None, :])
    ).astype(jnp.bfloat16)
    selector, weighted = lax.optimization_barrier((selector, weighted))
    local_source = jnp.dot(selector, weighted, preferred_element_type=jnp.float32)
    group_first = lax.axis_index("freq") * freqs_dev
    wave_numbers = wave_step * (
        (group_first + jnp.arange(freqs_dev, dtype=jnp.int32)).astype(jnp.float32) + 1.0
    )
    blocks = local_source.reshape(groups, panels_dev, columns)
    if groups & (groups - 1) == 0 and groups >= 4:
        bits = [1 << k for k in range(groups.bit_length() - 3)]
        own_source = halving_sum(blocks, bits)
        portion = doubling_gather(own_source, bits, groups).reshape(panel_total, columns)
    else:
        own_source = jnp.sum(lax.all_to_all(blocks, "obs", 0, 0, tiled=True), axis=0)
        portion = lax.all_to_all(
            jnp.broadcast_to(own_source[None], blocks.shape), "obs", 0, 0, tiled=True
        ).reshape(panel_total, columns)
    summed = far_field(portion, panel_position, observer_position, wave_numbers)
    pressure = summed * (reference_radius / math.sqrt(panel_total))
    energy = jnp.sum(pressure[:, 0] * pressure[:, 0] + pressure[:, 1] * pressure[:, 1], axis=0)
    if lax.axis_size("freq") == 2:
        band_total = energy + lax.ppermute(energy, "freq", [(0, 1), (1, 0)])
    else:
        band_total = lax.psum(energy, "freq")
    level = jnp.log(band_total / (freqs_dev * lax.axis_size("freq")) + 1e-06)
    return (pressure, level)


def solution(mesh):
    in_specs = (P("obs", "freq"), P("obs"), P("obs", None), P("obs"), P(), P(None, "obs"))
    out_specs = (P("freq", None, "obs"), P("obs"))
    return jax.shard_map(shards, mesh=mesh, in_specs=in_specs, out_specs=out_specs, check_vma=False)
```

```python
import functools
import math

import jax
import jax.numpy as jnp
from jax import lax
from jax.experimental import pallas as pl
from jax.experimental.pallas import tpu as pltpu
from jax.sharding import PartitionSpec as P

wave_step = 0.1
reference_radius = 10.0


def field_kernel(
    block_group, freq_unroll, low_chunks, wave_ref, geo_ref, low_ref, high_ref, out_ref, acc_ref, chan_ref, spread_ref
):
    freqs, _, observers, lanes = acc_ref.shape
    blocks = observers // 8

    @pl.when(pl.program_id(0) == 0)
    def _():
        acc_ref[...] = jnp.zeros(acc_ref.shape, acc_ref.dtype)

    chunk = pl.program_id(0)

    @pl.when(chunk < low_chunks)
    def _():
        chan_ref[...] = jnp.transpose(low_ref[...])

    @pl.when(chunk >= low_chunks)
    def _():
        chan_ref[...] = jnp.transpose(high_ref[...])

    def spread_body(row, carry):
        spread_ref[row] = jnp.broadcast_to(chan_ref[pl.ds(row, 1), :], (8, lanes))
        return carry

    lax.fori_loop(0, chan_ref.shape[0], spread_body, 0, unroll=8)

    def block_body(group, carry):
        spans = [
            pl.ds(pl.multiple_of((group * block_group + member) * 8, 8), 8)
            for member in range(block_group)
        ]
        step_cos = [geo_ref[2, rows, :] for rows in spans]
        step_sin = [geo_ref[3, rows, :] for rows in spans]
        along = [[geo_ref[4 + j, rows, :] for j in range(3)] for rows in spans]
        distance = [geo_ref[7, rows, :] for rows in spans]

        def freq_body(f, phase):
            base = f * 8
            channel = [spread_ref[base + c] for c in range(8)]
            wave = wave_ref[f]
            turned = []
            for member, rows in enumerate(spans):
                weight_real, weight_imag = phase[member]
                g = along[member]
                wave_distance = wave * distance[member]
                dipole_real = g[0] * channel[2] + g[1] * channel[4] + g[2] * channel[6]
                dipole_imag = g[0] * channel[3] + g[1] * channel[5] + g[2] * channel[7]
                amp_real = channel[0] + dipole_real - wave_distance * dipole_imag
                amp_imag = channel[1] + dipole_imag + wave_distance * dipole_real
                acc_ref[f, 0, rows, :] += weight_real * amp_real + weight_imag * amp_imag
                acc_ref[f, 1, rows, :] += weight_real * amp_imag - weight_imag * amp_real
                turned.append(
                    (
                        weight_real * step_cos[member] - weight_imag * step_sin[member],
                        weight_imag * step_cos[member] + weight_real * step_sin[member],
                    )
                )
            return tuple(turned)

        start = tuple((geo_ref[0, rows, :], geo_ref[1, rows, :]) for rows in spans)
        lax.fori_loop(0, freqs, freq_body, start, unroll=freq_unroll)
        return carry

    lax.fori_loop(0, blocks // block_group, block_body, 0)

    @pl.when(pl.program_id(0) == pl.num_programs(0) - 1)
    def _():
        flat = acc_ref[...].reshape(freqs * 2 * observers, lanes)
        spread = lax.broadcasted_iota(jnp.int32, (8, lanes), 1) // (lanes // 8)
        rows = lax.broadcasted_iota(jnp.int32, (8, lanes), 0)
        out_ref[...] = lax.dot_general(
            (spread == rows).astype(jnp.float32),
            flat,
            (((1,), (1,)), ((), ())),
            precision=lax.Precision.HIGHEST,
            preferred_element_type=jnp.float32,
        )


def far_field(low, high, panel_position, observer_position, wave_numbers):
    columns = low.shape[1]
    low_chunks = low.shape[0] // 128
    panel_total = low.shape[0] + high.shape[0]
    freqs = columns // 8
    observers = observer_position.shape[1]
    offsets = observer_position[:, :, None] - panel_position[:, None, :]
    distance = jnp.sqrt(offsets[0] * offsets[0] + offsets[1] * offsets[1] + offsets[2] * offsets[2])
    inverse = 1.0 / distance
    first_phase = wave_numbers[0] * distance
    step_phase = wave_step * distance
    geometry = jnp.stack(
        [
            jnp.cos(first_phase) * inverse,
            jnp.sin(first_phase) * inverse,
            jnp.cos(step_phase),
            jnp.sin(step_phase),
            offsets[0] * inverse * inverse,
            offsets[1] * inverse * inverse,
            offsets[2] * inverse * inverse,
            distance,
        ]
    )
    summed = pl.pallas_call(
        functools.partial(field_kernel, math.gcd(observers // 8, 4), 2, low_chunks),
        grid=(panel_total // 128,),
        in_specs=[
            pl.BlockSpec(memory_space=pltpu.SMEM),
            pl.BlockSpec((8, observers, 128), lambda chunk: (0, 0, chunk)),
            pl.BlockSpec((128, columns), lambda chunk: (jnp.minimum(chunk, low_chunks - 1), 0)),
            pl.BlockSpec((128, columns), lambda chunk: (jnp.maximum(chunk - low_chunks, 0), 0)),
        ],
        out_specs=pl.BlockSpec((8, freqs * 2 * observers), lambda chunk: (0, 0)),
        out_shape=jax.ShapeDtypeStruct((8, freqs * 2 * observers), jnp.float32),
        scratch_shapes=[
            pltpu.VMEM((freqs, 2, observers, 128), jnp.float32),
            pltpu.VMEM((columns, 128), jnp.float32),
            pltpu.VMEM((columns, 8, 128), jnp.float32),
        ],
        compiler_params=pltpu.CompilerParams(dimension_semantics=("arbitrary",)),
    )(wave_numbers, geometry, low, high)
    return jnp.sum(summed, axis=0).reshape(freqs, 2, observers)


def partner_pairs(groups, bit):
    return [(k, k ^ bit) for k in range(groups)]


def quad_pairs(groups, shift):
    low = groups // 4
    return [(k, ((k // low + shift) % 4) * low + k % low) for k in range(groups)]


def halving_sum(blocks, bits):
    groups = blocks.shape[0]
    place = lax.axis_index("obs")
    current = blocks
    for bit in bits:
        split = current.reshape((current.shape[0] // 2, 2) + current.shape[1:])
        mine = (place // bit) % 2
        keep = lax.dynamic_index_in_dim(split, mine, 1, keepdims=False)
        send = lax.dynamic_index_in_dim(split, 1 - mine, 1, keepdims=False)
        current = keep + lax.ppermute(send, "obs", partner_pairs(groups, bit))
    quarter = place // (groups // 4)
    total = lax.dynamic_index_in_dim(current, quarter, 0, keepdims=False)
    for shift in (1, 2, 3):
        piece = lax.dynamic_index_in_dim(current, (quarter + shift) % 4, 0, keepdims=False)
        total = total + lax.ppermute(piece, "obs", quad_pairs(groups, shift))
    return total


def doubling_gather(own, bits, groups):
    place = lax.axis_index("obs")
    quarter = place // (groups // 4)
    arrived = jnp.stack(
        [own] + [lax.ppermute(own, "obs", quad_pairs(groups, shift)) for shift in (1, 2, 3)]
    )
    gathered = jnp.stack(
        [lax.dynamic_index_in_dim(arrived, (quarter - k) % 4, 0, keepdims=False) for k in range(4)]
    )
    for bit in reversed(bits):
        mine = (place // bit) % 2
        other = lax.ppermute(gathered, "obs", partner_pairs(groups, bit))
        if bit == 1:
            return gathered, other
        low = jnp.where(mine == 0, gathered, other)
        high = jnp.where(mine == 0, other, gathered)
        gathered = jnp.stack([low, high], axis=1).reshape((-1,) + gathered.shape[1:])
    return gathered


def shards(cell_spectra, cell_weight, cell_owner, cell_local, panel_position, observer_position):
    cell_rows, columns = cell_spectra.shape
    freqs_dev = columns // 8
    groups = lax.axis_size("obs")
    panel_total = panel_position.shape[1]
    panels_dev = panel_total // groups
    weighted = (cell_weight[:, None] * cell_spectra.astype(jnp.float32)).astype(jnp.bfloat16)
    panel_number = jnp.arange(panel_total, dtype=jnp.int32)[:, None]
    selector = (
        (panel_number // panels_dev == cell_owner[:, 0][None, :])
        & (panel_number % panels_dev == cell_local[None, :])
    ).astype(jnp.bfloat16)
    local_source = jnp.dot(selector, weighted, preferred_element_type=jnp.float32)
    group_first = lax.axis_index("freq") * freqs_dev
    wave_numbers = wave_step * (
        (group_first + jnp.arange(freqs_dev, dtype=jnp.int32)).astype(jnp.float32) + 1.0
    )
    blocks = local_source.reshape(groups, panels_dev, columns)
    if groups & (groups - 1) == 0 and groups >= 8:
        bits = [1 << k for k in range(groups.bit_length() - 3)]
        own_source = halving_sum(blocks, bits)
        mine_half, other_half = doubling_gather(own_source, bits, groups)
        mine = lax.axis_index("obs") % 2
        paired = panel_position.reshape(3, groups // 2, 2, panels_dev)
        ordered = jnp.concatenate(
            [
                lax.dynamic_index_in_dim(paired, mine, 2, keepdims=False),
                lax.dynamic_index_in_dim(paired, 1 - mine, 2, keepdims=False),
            ],
            axis=1,
        ).reshape(3, panel_total)
        summed = far_field(
            mine_half.reshape(-1, columns),
            other_half.reshape(-1, columns),
            ordered,
            observer_position,
            wave_numbers,
        )
    else:
        own_source = jnp.sum(lax.all_to_all(blocks, "obs", 0, 0, tiled=True), axis=0)
        portion = lax.all_to_all(
            jnp.broadcast_to(own_source[None], blocks.shape), "obs", 0, 0, tiled=True
        ).reshape(panel_total, columns)
        half = panel_total // 256 * 128
        summed = far_field(portion[:half], portion[half:], panel_position, observer_position, wave_numbers)
    pressure = summed * (reference_radius / math.sqrt(panel_total))
    energy = jnp.sum(pressure[:, 0] * pressure[:, 0] + pressure[:, 1] * pressure[:, 1], axis=0)
    if lax.axis_size("freq") == 2:
        band_total = energy + lax.ppermute(energy, "freq", [(0, 1), (1, 0)])
    else:
        band_total = lax.psum(energy, "freq")
    level = jnp.log(band_total / (freqs_dev * lax.axis_size("freq")) + 1e-06)
    return (pressure, level)


def solution(mesh):
    in_specs = (P("obs", "freq"), P("obs"), P("obs", None), P("obs"), P(), P(None, "obs"))
    out_specs = (P("freq", None, "obs"), P("obs"))
    return jax.shard_map(shards, mesh=mesh, in_specs=in_specs, out_specs=out_specs, check_vma=False)
```

```python
import functools
import math

import jax
import jax.numpy as jnp
from jax import lax
from jax.experimental import pallas as pl
from jax.experimental.pallas import tpu as pltpu
from jax.sharding import PartitionSpec as P

wave_step = 0.1
reference_radius = 10.0


def field_kernel(block_group, freq_unroll, wave_ref, geo_ref, src_ref, out_ref, acc_ref, chan_ref):
    freqs, _, observers, lanes = acc_ref.shape
    blocks = observers // 8

    @pl.when(pl.program_id(0) == 0)
    def _():
        acc_ref[...] = jnp.zeros(acc_ref.shape, acc_ref.dtype)

    chan_ref[...] = jnp.transpose(src_ref[...])


    def block_body(group, carry):
        spans = [
            pl.ds(pl.multiple_of((group * block_group + member) * 8, 8), 8)
            for member in range(block_group)
        ]
        step_cos = [geo_ref[2, rows, :] for rows in spans]
        step_sin = [geo_ref[3, rows, :] for rows in spans]
        along = [[geo_ref[4 + j, rows, :] for j in range(3)] for rows in spans]
        distance = [geo_ref[7, rows, :] for rows in spans]

        def freq_body(f, phase):
            base = f * 8
            channel = [chan_ref[pl.ds(base + c, 8, stride=0), :] for c in range(8)]
            wave = wave_ref[f]
            turned = []
            for member, rows in enumerate(spans):
                weight_real, weight_imag = phase[member]
                g = along[member]
                wave_distance = wave * distance[member]
                dipole_real = g[0] * channel[2] + g[1] * channel[4] + g[2] * channel[6]
                dipole_imag = g[0] * channel[3] + g[1] * channel[5] + g[2] * channel[7]
                amp_real = channel[0] + dipole_real - wave_distance * dipole_imag
                amp_imag = channel[1] + dipole_imag + wave_distance * dipole_real
                acc_ref[f, 0, rows, :] += weight_real * amp_real + weight_imag * amp_imag
                acc_ref[f, 1, rows, :] += weight_real * amp_imag - weight_imag * amp_real
                turned.append(
                    (
                        weight_real * step_cos[member] - weight_imag * step_sin[member],
                        weight_imag * step_cos[member] + weight_real * step_sin[member],
                    )
                )
            return tuple(turned)

        start = tuple((geo_ref[0, rows, :], geo_ref[1, rows, :]) for rows in spans)
        lax.fori_loop(0, freqs, freq_body, start, unroll=freq_unroll)
        return carry

    lax.fori_loop(0, blocks // block_group, block_body, 0)

    @pl.when(pl.program_id(0) == pl.num_programs(0) - 1)
    def _():
        flat = acc_ref[...].reshape(freqs * 2 * observers, lanes)
        out_ref[...] = lax.dot_general(
            jnp.ones((8, lanes), jnp.float32),
            flat,
            (((1,), (1,)), ((), ())),
            precision=lax.Precision.HIGHEST,
            preferred_element_type=jnp.float32,
        )


def far_field(portion, panel_position, observer_position, wave_numbers):
    panel_total, columns = portion.shape
    freqs = columns // 8
    observers = observer_position.shape[1]
    offsets = observer_position[:, :, None] - panel_position[:, None, :]
    distance = jnp.sqrt(offsets[0] * offsets[0] + offsets[1] * offsets[1] + offsets[2] * offsets[2])
    inverse = 1.0 / distance
    first_phase = wave_numbers[0] * distance
    step_phase = wave_step * distance
    geometry = jnp.stack(
        [
            jnp.cos(first_phase) * inverse,
            jnp.sin(first_phase) * inverse,
            jnp.cos(step_phase),
            jnp.sin(step_phase),
            offsets[0] * inverse * inverse,
            offsets[1] * inverse * inverse,
            offsets[2] * inverse * inverse,
            distance,
        ]
    )
    summed = pl.pallas_call(
        functools.partial(field_kernel, math.gcd(observers // 8, 4), 4),
        grid=(panel_total // 128,),
        in_specs=[
            pl.BlockSpec(memory_space=pltpu.SMEM),
            pl.BlockSpec((8, observers, 128), lambda chunk: (0, 0, chunk)),
            pl.BlockSpec((128, columns), lambda chunk: (chunk, 0)),
        ],
        out_specs=pl.BlockSpec((8, freqs * 2 * observers), lambda chunk: (0, 0)),
        out_shape=jax.ShapeDtypeStruct((8, freqs * 2 * observers), jnp.float32),
        scratch_shapes=[
            pltpu.VMEM((freqs, 2, observers, 128), jnp.float32),
            pltpu.VMEM((columns, 128), jnp.float32),
        ],
        compiler_params=pltpu.CompilerParams(dimension_semantics=("arbitrary",)),
    )(wave_numbers, geometry, portion)
    return summed[0].reshape(freqs, 2, observers)


def partner_pairs(groups, bit):
    return [(k, k ^ bit) for k in range(groups)]


def quad_pairs(groups, shift):
    low = groups // 4
    return [(k, ((k // low + shift) % 4) * low + k % low) for k in range(groups)]


def halving_sum(blocks, bits):
    groups = blocks.shape[0]
    place = lax.axis_index("obs")
    current = blocks
    for bit in bits:
        split = current.reshape((current.shape[0] // 2, 2) + current.shape[1:])
        mine = (place // bit) % 2
        keep = lax.dynamic_index_in_dim(split, mine, 1, keepdims=False)
        send = lax.dynamic_index_in_dim(split, 1 - mine, 1, keepdims=False)
        current = keep + lax.ppermute(send, "obs", partner_pairs(groups, bit))
    quarter = place // (groups // 4)
    total = lax.dynamic_index_in_dim(current, quarter, 0, keepdims=False)
    for shift in (1, 2, 3):
        piece = lax.dynamic_index_in_dim(current, (quarter + shift) % 4, 0, keepdims=False)
        total = total + lax.ppermute(piece, "obs", quad_pairs(groups, shift))
    return total


def doubling_gather(own, bits, groups):
    place = lax.axis_index("obs")
    quarter = place // (groups // 4)
    arrived = jnp.stack(
        [own] + [lax.ppermute(own, "obs", quad_pairs(groups, shift)) for shift in (1, 2, 3)]
    )
    gathered = jnp.stack(
        [lax.dynamic_index_in_dim(arrived, (quarter - k) % 4, 0, keepdims=False) for k in range(4)]
    )
    for bit in reversed(bits):
        mine = (place // bit) % 2
        other = lax.ppermute(gathered, "obs", partner_pairs(groups, bit))
        low = jnp.where(mine == 0, gathered, other)
        high = jnp.where(mine == 0, other, gathered)
        gathered = jnp.stack([low, high], axis=1).reshape((-1,) + gathered.shape[1:])
    return gathered


def shards(cell_spectra, cell_weight, cell_owner, cell_local, panel_position, observer_position):
    cell_rows, columns = cell_spectra.shape
    freqs_dev = columns // 8
    groups = lax.axis_size("obs")
    panel_total = panel_position.shape[1]
    panels_dev = panel_total // groups
    weighted = (cell_weight[:, None] * cell_spectra.astype(jnp.float32)).astype(jnp.bfloat16)
    panel_number = jnp.arange(panel_total, dtype=jnp.int32)[:, None]
    selector = (
        (panel_number // panels_dev == cell_owner[:, 0][None, :])
        & (panel_number % panels_dev == cell_local[None, :])
    ).astype(jnp.bfloat16)
    local_source = jnp.dot(selector, weighted, preferred_element_type=jnp.float32)
    group_first = lax.axis_index("freq") * freqs_dev
    wave_numbers = wave_step * (
        (group_first + jnp.arange(freqs_dev, dtype=jnp.int32)).astype(jnp.float32) + 1.0
    )
    blocks = local_source.reshape(groups, panels_dev, columns)
    if groups & (groups - 1) == 0 and groups >= 4:
        bits = [1 << k for k in range(groups.bit_length() - 3)]
        own_source = halving_sum(blocks, bits)
        portion = doubling_gather(own_source, bits, groups).reshape(panel_total, columns)
    else:
        own_source = jnp.sum(lax.all_to_all(blocks, "obs", 0, 0, tiled=True), axis=0)
        portion = lax.all_to_all(
            jnp.broadcast_to(own_source[None], blocks.shape), "obs", 0, 0, tiled=True
        ).reshape(panel_total, columns)
    summed = far_field(portion, panel_position, observer_position, wave_numbers)
    pressure = summed * (reference_radius / math.sqrt(panel_total))
    energy = jnp.sum(pressure[:, 0] * pressure[:, 0] + pressure[:, 1] * pressure[:, 1], axis=0)
    if lax.axis_size("freq") == 2:
        band_total = energy + lax.ppermute(energy, "freq", [(0, 1), (1, 0)])
    else:
        band_total = lax.psum(energy, "freq")
    level = jnp.log(band_total / (freqs_dev * lax.axis_size("freq")) + 1e-06)
    return (pressure, level)


def solution(mesh):
    in_specs = (P("obs", "freq"), P("obs"), P("obs", None), P("obs"), P(), P(None, "obs"))
    out_specs = (P("freq", None, "obs"), P("obs"))
    return jax.shard_map(shards, mesh=mesh, in_specs=in_specs, out_specs=out_specs, check_vma=False)
```

```python
import functools
import math

import jax
import jax.numpy as jnp
from jax import lax
from jax.experimental import pallas as pl
from jax.experimental.pallas import tpu as pltpu
from jax.sharding import PartitionSpec as P

wave_step = 0.1
reference_radius = 10.0


def field_kernel(block_group, freq_unroll, wave_ref, geo_ref, src_ref, out_ref, acc_ref, chan_ref):
    freqs, _, observers, lanes = acc_ref.shape
    blocks = observers // 8


    chan_ref[...] = jnp.transpose(src_ref[...])


    def sweep(first):
        def block_body(group, carry):
            spans = [
                pl.ds(pl.multiple_of((group * block_group + member) * 8, 8), 8)
                for member in range(block_group)
            ]
            step_cos = [geo_ref[2, rows, :] for rows in spans]
            step_sin = [geo_ref[3, rows, :] for rows in spans]
            along = [[geo_ref[4 + j, rows, :] for j in range(3)] for rows in spans]
            distance = [geo_ref[7, rows, :] for rows in spans]

            def freq_body(f, phase):
                base = f * 8
                channel = [chan_ref[pl.ds(base + c, 8, stride=0), :] for c in range(8)]
                wave = wave_ref[f]
                turned = []
                for member, rows in enumerate(spans):
                    weight_real, weight_imag = phase[member]
                    g = along[member]
                    wave_distance = wave * distance[member]
                    dipole_real = g[0] * channel[2] + g[1] * channel[4] + g[2] * channel[6]
                    dipole_imag = g[0] * channel[3] + g[1] * channel[5] + g[2] * channel[7]
                    amp_real = channel[0] + dipole_real - wave_distance * dipole_imag
                    amp_imag = channel[1] + dipole_imag + wave_distance * dipole_real
                    real_term = weight_real * amp_real + weight_imag * amp_imag
                    imag_term = weight_real * amp_imag - weight_imag * amp_real
                    if first:
                        acc_ref[f, 0, rows, :] = real_term
                        acc_ref[f, 1, rows, :] = imag_term
                    else:
                        acc_ref[f, 0, rows, :] += real_term
                        acc_ref[f, 1, rows, :] += imag_term
                    turned.append(
                        (
                            weight_real * step_cos[member] - weight_imag * step_sin[member],
                            weight_imag * step_cos[member] + weight_real * step_sin[member],
                        )
                    )
                return tuple(turned)

            start = tuple((geo_ref[0, rows, :], geo_ref[1, rows, :]) for rows in spans)
            lax.fori_loop(0, freqs, freq_body, start, unroll=freq_unroll)
            return carry

        lax.fori_loop(0, blocks // block_group, block_body, 0)

    @pl.when(pl.program_id(0) == 0)
    def _():
        sweep(True)

    @pl.when(pl.program_id(0) > 0)
    def _():
        sweep(False)

    @pl.when(pl.program_id(0) == pl.num_programs(0) - 1)
    def _():
        flat = acc_ref[...].reshape(freqs * 2 * observers, lanes)
        out_ref[...] = lax.dot_general(
            jnp.ones((8, lanes), jnp.float32),
            flat,
            (((1,), (1,)), ((), ())),
            precision=lax.Precision.HIGHEST,
            preferred_element_type=jnp.float32,
        )


def far_field(portion, panel_position, observer_position, wave_numbers):
    panel_total, columns = portion.shape
    freqs = columns // 8
    observers = observer_position.shape[1]
    offsets = observer_position[:, :, None] - panel_position[:, None, :]
    distance = jnp.sqrt(offsets[0] * offsets[0] + offsets[1] * offsets[1] + offsets[2] * offsets[2])
    inverse = 1.0 / distance
    first_phase = wave_numbers[0] * distance
    step_phase = wave_step * distance
    geometry = jnp.stack(
        [
            jnp.cos(first_phase) * inverse,
            jnp.sin(first_phase) * inverse,
            jnp.cos(step_phase),
            jnp.sin(step_phase),
            offsets[0] * inverse * inverse,
            offsets[1] * inverse * inverse,
            offsets[2] * inverse * inverse,
            distance,
        ]
    )
    summed = pl.pallas_call(
        functools.partial(field_kernel, math.gcd(observers // 8, 4), 4),
        grid=(panel_total // 128,),
        in_specs=[
            pl.BlockSpec(memory_space=pltpu.SMEM),
            pl.BlockSpec((8, observers, 128), lambda chunk: (0, 0, chunk)),
            pl.BlockSpec((128, columns), lambda chunk: (chunk, 0)),
        ],
        out_specs=pl.BlockSpec((8, freqs * 2 * observers), lambda chunk: (0, 0)),
        out_shape=jax.ShapeDtypeStruct((8, freqs * 2 * observers), jnp.float32),
        scratch_shapes=[
            pltpu.VMEM((freqs, 2, observers, 128), jnp.float32),
            pltpu.VMEM((columns, 128), jnp.float32),
        ],
        compiler_params=pltpu.CompilerParams(dimension_semantics=("arbitrary",)),
    )(wave_numbers, geometry, portion)
    return summed[0].reshape(freqs, 2, observers)


def partner_pairs(groups, bit):
    return [(k, k ^ bit) for k in range(groups)]


def quad_pairs(groups, shift):
    low = groups // 4
    return [(k, ((k // low + shift) % 4) * low + k % low) for k in range(groups)]


def halving_sum(blocks, bits):
    groups = blocks.shape[0]
    place = lax.axis_index("obs")
    current = blocks
    for bit in bits:
        split = current.reshape((current.shape[0] // 2, 2) + current.shape[1:])
        mine = (place // bit) % 2
        keep = lax.dynamic_index_in_dim(split, mine, 1, keepdims=False)
        send = lax.dynamic_index_in_dim(split, 1 - mine, 1, keepdims=False)
        current = keep + lax.ppermute(send, "obs", partner_pairs(groups, bit))
    quarter = place // (groups // 4)
    total = lax.dynamic_index_in_dim(current, quarter, 0, keepdims=False)
    for shift in (1, 2, 3):
        piece = lax.dynamic_index_in_dim(current, (quarter + shift) % 4, 0, keepdims=False)
        total = total + lax.ppermute(piece, "obs", quad_pairs(groups, shift))
    return total


def doubling_gather(own, bits, groups):
    place = lax.axis_index("obs")
    quarter = place // (groups // 4)
    arrived = jnp.stack(
        [own] + [lax.ppermute(own, "obs", quad_pairs(groups, shift)) for shift in (1, 2, 3)]
    )
    gathered = jnp.stack(
        [lax.dynamic_index_in_dim(arrived, (quarter - k) % 4, 0, keepdims=False) for k in range(4)]
    )
    for bit in reversed(bits):
        mine = (place // bit) % 2
        other = lax.ppermute(gathered, "obs", partner_pairs(groups, bit))
        low = jnp.where(mine == 0, gathered, other)
        high = jnp.where(mine == 0, other, gathered)
        gathered = jnp.stack([low, high], axis=1).reshape((-1,) + gathered.shape[1:])
    return gathered


def shards(cell_spectra, cell_weight, cell_owner, cell_local, panel_position, observer_position):
    cell_rows, columns = cell_spectra.shape
    freqs_dev = columns // 8
    groups = lax.axis_size("obs")
    panel_total = panel_position.shape[1]
    panels_dev = panel_total // groups
    weighted = (cell_weight[:, None] * cell_spectra.astype(jnp.float32)).astype(jnp.bfloat16)
    panel_number = jnp.arange(panel_total, dtype=jnp.int32)[:, None]
    selector = (
        (panel_number // panels_dev == cell_owner[:, 0][None, :])
        & (panel_number % panels_dev == cell_local[None, :])
    ).astype(jnp.bfloat16)
    local_source = jnp.dot(selector, weighted, preferred_element_type=jnp.float32)
    group_first = lax.axis_index("freq") * freqs_dev
    wave_numbers = wave_step * (
        (group_first + jnp.arange(freqs_dev, dtype=jnp.int32)).astype(jnp.float32) + 1.0
    )
    blocks = local_source.reshape(groups, panels_dev, columns)
    if groups & (groups - 1) == 0 and groups >= 4:
        bits = [1 << k for k in range(groups.bit_length() - 3)]
        own_source = halving_sum(blocks, bits)
        portion = doubling_gather(own_source, bits, groups).reshape(panel_total, columns)
    else:
        own_source = jnp.sum(lax.all_to_all(blocks, "obs", 0, 0, tiled=True), axis=0)
        portion = lax.all_to_all(
            jnp.broadcast_to(own_source[None], blocks.shape), "obs", 0, 0, tiled=True
        ).reshape(panel_total, columns)
    summed = far_field(portion, panel_position, observer_position, wave_numbers)
    pressure = summed * (reference_radius / math.sqrt(panel_total))
    energy = jnp.sum(pressure[:, 0] * pressure[:, 0] + pressure[:, 1] * pressure[:, 1], axis=0)
    if lax.axis_size("freq") == 2:
        band_total = energy + lax.ppermute(energy, "freq", [(0, 1), (1, 0)])
    else:
        band_total = lax.psum(energy, "freq")
    level = jnp.log(band_total / (freqs_dev * lax.axis_size("freq")) + 1e-06)
    return (pressure, level)


def solution(mesh):
    in_specs = (P("obs", "freq"), P("obs"), P("obs", None), P("obs"), P(), P(None, "obs"))
    out_specs = (P("freq", None, "obs"), P("obs"))
    return jax.shard_map(shards, mesh=mesh, in_specs=in_specs, out_specs=out_specs, check_vma=False)
```

```python
import functools
import math

import jax
import jax.numpy as jnp
from jax import lax
from jax.experimental import pallas as pl
from jax.experimental.pallas import tpu as pltpu
from jax.sharding import PartitionSpec as P

wave_step = 0.1
reference_radius = 10.0


def field_kernel(
    block_group, freq_unroll, low_chunks, wave_ref, geo_ref, low_ref, high_ref, out_ref, acc_ref, chan_ref
):
    freqs, _, observers, lanes = acc_ref.shape
    blocks = observers // 8

    @pl.when(pl.program_id(0) == 0)
    def _():
        acc_ref[...] = jnp.zeros(acc_ref.shape, acc_ref.dtype)

    chunk = pl.program_id(0)

    @pl.when(chunk < low_chunks)
    def _():
        chan_ref[...] = jnp.transpose(low_ref[...])

    @pl.when(chunk >= low_chunks)
    def _():
        chan_ref[...] = jnp.transpose(high_ref[...])


    def block_body(group, carry):
        spans = [
            pl.ds(pl.multiple_of((group * block_group + member) * 8, 8), 8)
            for member in range(block_group)
        ]
        step_cos = [geo_ref[2, rows, :] for rows in spans]
        step_sin = [geo_ref[3, rows, :] for rows in spans]
        along = [[geo_ref[4 + j, rows, :] for j in range(3)] for rows in spans]
        distance = [geo_ref[7, rows, :] for rows in spans]

        def freq_body(f, phase):
            base = f * 8
            channel = [chan_ref[pl.ds(base + c, 8, stride=0), :] for c in range(8)]
            wave = wave_ref[f]
            turned = []
            for member, rows in enumerate(spans):
                weight_real, weight_imag = phase[member]
                g = along[member]
                wave_distance = wave * distance[member]
                dipole_real = g[0] * channel[2] + g[1] * channel[4] + g[2] * channel[6]
                dipole_imag = g[0] * channel[3] + g[1] * channel[5] + g[2] * channel[7]
                amp_real = channel[0] + dipole_real - wave_distance * dipole_imag
                amp_imag = channel[1] + dipole_imag + wave_distance * dipole_real
                acc_ref[f, 0, rows, :] += weight_real * amp_real + weight_imag * amp_imag
                acc_ref[f, 1, rows, :] += weight_real * amp_imag - weight_imag * amp_real
                turned.append(
                    (
                        weight_real * step_cos[member] - weight_imag * step_sin[member],
                        weight_imag * step_cos[member] + weight_real * step_sin[member],
                    )
                )
            return tuple(turned)

        start = tuple((geo_ref[0, rows, :], geo_ref[1, rows, :]) for rows in spans)
        lax.fori_loop(0, freqs, freq_body, start, unroll=freq_unroll)
        return carry

    lax.fori_loop(0, blocks // block_group, block_body, 0)

    @pl.when(pl.program_id(0) == pl.num_programs(0) - 1)
    def _():
        flat = acc_ref[...].reshape(freqs * 2 * observers, lanes)
        out_ref[...] = lax.dot_general(
            jnp.ones((8, lanes), jnp.float32),
            flat,
            (((1,), (1,)), ((), ())),
            precision=lax.Precision.HIGHEST,
            preferred_element_type=jnp.float32,
        )


def far_field(low, high, panel_position, observer_position, wave_numbers):
    columns = low.shape[1]
    low_chunks = low.shape[0] // 128
    panel_total = low.shape[0] + high.shape[0]
    freqs = columns // 8
    observers = observer_position.shape[1]
    offsets = observer_position[:, :, None] - panel_position[:, None, :]
    distance = jnp.sqrt(offsets[0] * offsets[0] + offsets[1] * offsets[1] + offsets[2] * offsets[2])
    inverse = 1.0 / distance
    first_phase = wave_numbers[0] * distance
    step_phase = wave_step * distance
    geometry = jnp.stack(
        [
            jnp.cos(first_phase) * inverse,
            jnp.sin(first_phase) * inverse,
            jnp.cos(step_phase),
            jnp.sin(step_phase),
            offsets[0] * inverse * inverse,
            offsets[1] * inverse * inverse,
            offsets[2] * inverse * inverse,
            distance,
        ]
    )
    summed = pl.pallas_call(
        functools.partial(field_kernel, math.gcd(observers // 8, 4), 4, low_chunks),
        grid=(panel_total // 128,),
        in_specs=[
            pl.BlockSpec(memory_space=pltpu.SMEM),
            pl.BlockSpec((8, observers, 128), lambda chunk: (0, 0, chunk)),
            pl.BlockSpec((128, columns), lambda chunk: (jnp.minimum(chunk, low_chunks - 1), 0)),
            pl.BlockSpec((128, columns), lambda chunk: (jnp.maximum(chunk - low_chunks, 0), 0)),
        ],
        out_specs=pl.BlockSpec((8, freqs * 2 * observers), lambda chunk: (0, 0)),
        out_shape=jax.ShapeDtypeStruct((8, freqs * 2 * observers), jnp.float32),
        scratch_shapes=[
            pltpu.VMEM((freqs, 2, observers, 128), jnp.float32),
            pltpu.VMEM((columns, 128), jnp.float32),
        ],
        compiler_params=pltpu.CompilerParams(dimension_semantics=("arbitrary",)),
    )(wave_numbers, geometry, low, high)
    return summed[0].reshape(freqs, 2, observers)


def partner_pairs(groups, bit):
    return [(k, k ^ bit) for k in range(groups)]


def quad_pairs(groups, shift):
    low = groups // 4
    return [(k, ((k // low + shift) % 4) * low + k % low) for k in range(groups)]


def halving_sum(blocks, bits):
    groups = blocks.shape[0]
    place = lax.axis_index("obs")
    current = blocks
    for bit in bits:
        split = current.reshape((current.shape[0] // 2, 2) + current.shape[1:])
        mine = (place // bit) % 2
        keep = lax.dynamic_index_in_dim(split, mine, 1, keepdims=False)
        send = lax.dynamic_index_in_dim(split, 1 - mine, 1, keepdims=False)
        current = keep + lax.ppermute(send, "obs", partner_pairs(groups, bit))
    quarter = place // (groups // 4)
    total = lax.dynamic_index_in_dim(current, quarter, 0, keepdims=False)
    for shift in (1, 2, 3):
        piece = lax.dynamic_index_in_dim(current, (quarter + shift) % 4, 0, keepdims=False)
        total = total + lax.ppermute(piece, "obs", quad_pairs(groups, shift))
    return total


def doubling_gather(own, bits, groups):
    place = lax.axis_index("obs")
    quarter = place // (groups // 4)
    arrived = jnp.stack(
        [own] + [lax.ppermute(own, "obs", quad_pairs(groups, shift)) for shift in (1, 2, 3)]
    )
    gathered = jnp.stack(
        [lax.dynamic_index_in_dim(arrived, (quarter - k) % 4, 0, keepdims=False) for k in range(4)]
    )
    for bit in reversed(bits):
        mine = (place // bit) % 2
        other = lax.ppermute(gathered, "obs", partner_pairs(groups, bit))
        if bit == 1:
            return gathered, other
        low = jnp.where(mine == 0, gathered, other)
        high = jnp.where(mine == 0, other, gathered)
        gathered = jnp.stack([low, high], axis=1).reshape((-1,) + gathered.shape[1:])
    return gathered


def shards(cell_spectra, cell_weight, cell_owner, cell_local, panel_position, observer_position):
    cell_rows, columns = cell_spectra.shape
    freqs_dev = columns // 8
    groups = lax.axis_size("obs")
    panel_total = panel_position.shape[1]
    panels_dev = panel_total // groups
    weighted = (cell_weight[:, None] * cell_spectra.astype(jnp.float32)).astype(jnp.bfloat16)
    panel_number = jnp.arange(panel_total, dtype=jnp.int32)[:, None]
    selector = (
        (panel_number // panels_dev == cell_owner[:, 0][None, :])
        & (panel_number % panels_dev == cell_local[None, :])
    ).astype(jnp.bfloat16)
    local_source = jnp.dot(selector, weighted, preferred_element_type=jnp.float32)
    group_first = lax.axis_index("freq") * freqs_dev
    wave_numbers = wave_step * (
        (group_first + jnp.arange(freqs_dev, dtype=jnp.int32)).astype(jnp.float32) + 1.0
    )
    blocks = local_source.reshape(groups, panels_dev, columns)
    if groups & (groups - 1) == 0 and groups >= 8:
        bits = [1 << k for k in range(groups.bit_length() - 3)]
        own_source = halving_sum(blocks, bits)
        mine_half, other_half = doubling_gather(own_source, bits, groups)
        mine = lax.axis_index("obs") % 2
        paired = panel_position.reshape(3, groups // 2, 2, panels_dev)
        ordered = jnp.concatenate(
            [
                lax.dynamic_index_in_dim(paired, mine, 2, keepdims=False),
                lax.dynamic_index_in_dim(paired, 1 - mine, 2, keepdims=False),
            ],
            axis=1,
        ).reshape(3, panel_total)
        summed = far_field(
            mine_half.reshape(-1, columns),
            other_half.reshape(-1, columns),
            ordered,
            observer_position,
            wave_numbers,
        )
    else:
        own_source = jnp.sum(lax.all_to_all(blocks, "obs", 0, 0, tiled=True), axis=0)
        portion = lax.all_to_all(
            jnp.broadcast_to(own_source[None], blocks.shape), "obs", 0, 0, tiled=True
        ).reshape(panel_total, columns)
        half = panel_total // 256 * 128
        summed = far_field(portion[:half], portion[half:], panel_position, observer_position, wave_numbers)
    pressure = summed * (reference_radius / math.sqrt(panel_total))
    energy = jnp.sum(pressure[:, 0] * pressure[:, 0] + pressure[:, 1] * pressure[:, 1], axis=0)
    if lax.axis_size("freq") == 2:
        band_total = energy + lax.ppermute(energy, "freq", [(0, 1), (1, 0)])
    else:
        band_total = lax.psum(energy, "freq")
    level = jnp.log(band_total / (freqs_dev * lax.axis_size("freq")) + 1e-06)
    return (pressure, level)


def solution(mesh):
    in_specs = (P("obs", "freq"), P("obs"), P("obs", None), P("obs"), P(), P(None, "obs"))
    out_specs = (P("freq", None, "obs"), P("obs"))
    return jax.shard_map(shards, mesh=mesh, in_specs=in_specs, out_specs=out_specs, check_vma=False)
```

```python
import functools
import math

import jax
import jax.numpy as jnp
from jax import lax
from jax.experimental import pallas as pl
from jax.experimental.pallas import tpu as pltpu
from jax.sharding import PartitionSpec as P

wave_step = 0.1
reference_radius = 10.0


def field_kernel(block_group, freq_unroll, wave_ref, geo_ref, src_ref, out_ref, acc_ref, chan_ref):
    freqs, _, observers, lanes = acc_ref.shape
    blocks = observers // 8

    @pl.when(pl.program_id(0) == 0)
    def _():
        acc_ref[...] = jnp.zeros(acc_ref.shape, acc_ref.dtype)

    chan_ref[...] = jnp.transpose(src_ref[...])


    def block_body(group, carry):
        spans = [
            pl.ds(pl.multiple_of((group * block_group + member) * 8, 8), 8)
            for member in range(block_group)
        ]
        step_cos = [geo_ref[2, rows, :] for rows in spans]
        step_sin = [geo_ref[3, rows, :] for rows in spans]
        along = [[geo_ref[4 + j, rows, :] for j in range(3)] for rows in spans]
        distance = [geo_ref[7, rows, :] for rows in spans]

        def freq_body(f, phase):
            base = f * 8
            channel = [chan_ref[pl.ds(base + c, 8, stride=0), :] for c in range(8)]
            wave = wave_ref[f]
            turned = []
            for member, rows in enumerate(spans):
                weight_real, weight_imag = phase[member]
                g = along[member]
                wave_distance = wave * distance[member]
                dipole_real = g[0] * channel[2] + g[1] * channel[4] + g[2] * channel[6]
                dipole_imag = g[0] * channel[3] + g[1] * channel[5] + g[2] * channel[7]
                amp_real = channel[0] + dipole_real - wave_distance * dipole_imag
                amp_imag = channel[1] + dipole_imag + wave_distance * dipole_real
                acc_ref[f, 0, rows, :] += weight_real * amp_real + weight_imag * amp_imag
                acc_ref[f, 1, rows, :] += weight_real * amp_imag - weight_imag * amp_real
                turned.append(
                    (
                        weight_real * step_cos[member] - weight_imag * step_sin[member],
                        weight_imag * step_cos[member] + weight_real * step_sin[member],
                    )
                )
            return tuple(turned)

        start = tuple((geo_ref[0, rows, :], geo_ref[1, rows, :]) for rows in spans)
        lax.fori_loop(0, freqs, freq_body, start, unroll=freq_unroll)
        return carry

    lax.fori_loop(0, blocks // block_group, block_body, 0)

    @pl.when(pl.program_id(0) == pl.num_programs(0) - 1)
    def _():
        flat = acc_ref[...].reshape(freqs * 2 * observers, lanes)
        out_ref[...] = lax.dot_general(
            jnp.ones((8, lanes), jnp.float32),
            flat,
            (((1,), (1,)), ((), ())),
            precision=lax.Precision.HIGH,
            preferred_element_type=jnp.float32,
        )


def far_field(portion, panel_position, observer_position, wave_numbers):
    panel_total, columns = portion.shape
    freqs = columns // 8
    observers = observer_position.shape[1]
    offsets = observer_position[:, :, None] - panel_position[:, None, :]
    distance = jnp.sqrt(offsets[0] * offsets[0] + offsets[1] * offsets[1] + offsets[2] * offsets[2])
    inverse = 1.0 / distance
    first_phase = wave_numbers[0] * distance
    step_phase = wave_step * distance
    geometry = jnp.stack(
        [
            jnp.cos(first_phase) * inverse,
            jnp.sin(first_phase) * inverse,
            jnp.cos(step_phase),
            jnp.sin(step_phase),
            offsets[0] * inverse * inverse,
            offsets[1] * inverse * inverse,
            offsets[2] * inverse * inverse,
            distance,
        ]
    )
    summed = pl.pallas_call(
        functools.partial(field_kernel, math.gcd(observers // 8, 4), 4),
        grid=(panel_total // 128,),
        in_specs=[
            pl.BlockSpec(memory_space=pltpu.SMEM),
            pl.BlockSpec((8, observers, 128), lambda chunk: (0, 0, chunk)),
            pl.BlockSpec((128, columns), lambda chunk: (chunk, 0)),
        ],
        out_specs=pl.BlockSpec((8, freqs * 2 * observers), lambda chunk: (0, 0)),
        out_shape=jax.ShapeDtypeStruct((8, freqs * 2 * observers), jnp.float32),
        scratch_shapes=[
            pltpu.VMEM((freqs, 2, observers, 128), jnp.float32),
            pltpu.VMEM((columns, 128), jnp.float32),
        ],
        compiler_params=pltpu.CompilerParams(dimension_semantics=("arbitrary",)),
    )(wave_numbers, geometry, portion)
    return summed[0].reshape(freqs, 2, observers)


def partner_pairs(groups, bit):
    return [(k, k ^ bit) for k in range(groups)]


def quad_pairs(groups, shift):
    low = groups // 4
    return [(k, ((k // low + shift) % 4) * low + k % low) for k in range(groups)]


def halving_sum(blocks, bits):
    groups = blocks.shape[0]
    place = lax.axis_index("obs")
    current = blocks
    for bit in bits:
        split = current.reshape((current.shape[0] // 2, 2) + current.shape[1:])
        mine = (place // bit) % 2
        keep = lax.dynamic_index_in_dim(split, mine, 1, keepdims=False)
        send = lax.dynamic_index_in_dim(split, 1 - mine, 1, keepdims=False)
        current = keep + lax.ppermute(send, "obs", partner_pairs(groups, bit))
    quarter = place // (groups // 4)
    total = lax.dynamic_index_in_dim(current, quarter, 0, keepdims=False)
    for shift in (1, 2, 3):
        piece = lax.dynamic_index_in_dim(current, (quarter + shift) % 4, 0, keepdims=False)
        total = total + lax.ppermute(piece, "obs", quad_pairs(groups, shift))
    return total


def doubling_gather(own, bits, groups):
    place = lax.axis_index("obs")
    quarter = place // (groups // 4)
    arrived = jnp.stack(
        [own] + [lax.ppermute(own, "obs", quad_pairs(groups, shift)) for shift in (1, 2, 3)]
    )
    gathered = jnp.stack(
        [lax.dynamic_index_in_dim(arrived, (quarter - k) % 4, 0, keepdims=False) for k in range(4)]
    )
    for bit in reversed(bits):
        mine = (place // bit) % 2
        other = lax.ppermute(gathered, "obs", partner_pairs(groups, bit))
        low = jnp.where(mine == 0, gathered, other)
        high = jnp.where(mine == 0, other, gathered)
        gathered = jnp.stack([low, high], axis=1).reshape((-1,) + gathered.shape[1:])
    return gathered


def shards(cell_spectra, cell_weight, cell_owner, cell_local, panel_position, observer_position):
    cell_rows, columns = cell_spectra.shape
    freqs_dev = columns // 8
    groups = lax.axis_size("obs")
    panel_total = panel_position.shape[1]
    panels_dev = panel_total // groups
    weighted = (cell_weight[:, None] * cell_spectra.astype(jnp.float32)).astype(jnp.bfloat16)
    panel_number = jnp.arange(panel_total, dtype=jnp.int32)[:, None]
    selector = (
        (panel_number // panels_dev == cell_owner[:, 0][None, :])
        & (panel_number % panels_dev == cell_local[None, :])
    ).astype(jnp.bfloat16)
    local_source = jnp.dot(selector, weighted, preferred_element_type=jnp.float32)
    group_first = lax.axis_index("freq") * freqs_dev
    wave_numbers = wave_step * (
        (group_first + jnp.arange(freqs_dev, dtype=jnp.int32)).astype(jnp.float32) + 1.0
    )
    blocks = local_source.reshape(groups, panels_dev, columns)
    if groups & (groups - 1) == 0 and groups >= 4:
        bits = [1 << k for k in range(groups.bit_length() - 3)]
        own_source = halving_sum(blocks, bits)
        portion = doubling_gather(own_source, bits, groups).reshape(panel_total, columns)
    else:
        own_source = jnp.sum(lax.all_to_all(blocks, "obs", 0, 0, tiled=True), axis=0)
        portion = lax.all_to_all(
            jnp.broadcast_to(own_source[None], blocks.shape), "obs", 0, 0, tiled=True
        ).reshape(panel_total, columns)
    summed = far_field(portion, panel_position, observer_position, wave_numbers)
    pressure = summed * (reference_radius / math.sqrt(panel_total))
    energy = jnp.sum(pressure[:, 0] * pressure[:, 0] + pressure[:, 1] * pressure[:, 1], axis=0)
    if lax.axis_size("freq") == 2:
        band_total = energy + lax.ppermute(energy, "freq", [(0, 1), (1, 0)])
    else:
        band_total = lax.psum(energy, "freq")
    level = jnp.log(band_total / (freqs_dev * lax.axis_size("freq")) + 1e-06)
    return (pressure, level)


def solution(mesh):
    in_specs = (P("obs", "freq"), P("obs"), P("obs", None), P("obs"), P(), P(None, "obs"))
    out_specs = (P("freq", None, "obs"), P("obs"))
    return jax.shard_map(shards, mesh=mesh, in_specs=in_specs, out_specs=out_specs, check_vma=False)
```

```python
import functools
import math

import jax
import jax.numpy as jnp
from jax import lax
from jax.experimental import pallas as pl
from jax.experimental.pallas import tpu as pltpu
from jax.sharding import PartitionSpec as P

wave_step = 0.1
reference_radius = 10.0


def field_kernel(block_group, freq_unroll, wave_ref, geo_ref, src_ref, out_ref, acc_ref, chan_ref):
    freqs, _, observers, lanes = acc_ref.shape
    blocks = observers // 8

    @pl.when(pl.program_id(0) == 0)
    def _():
        acc_ref[...] = jnp.zeros(acc_ref.shape, acc_ref.dtype)

    chan_ref[...] = jnp.transpose(src_ref[...])


    def block_body(group, carry):
        spans = [
            pl.ds(pl.multiple_of((group * block_group + member) * 8, 8), 8)
            for member in range(block_group)
        ]
        step_cos = [geo_ref[2, rows, :] for rows in spans]
        step_sin = [geo_ref[3, rows, :] for rows in spans]
        along = [[geo_ref[4 + j, rows, :] for j in range(3)] for rows in spans]
        distance = [geo_ref[7, rows, :] for rows in spans]

        def freq_body(f, phase):
            base = f * 8
            channel = [chan_ref[pl.ds(base + c, 8, stride=0), :] for c in range(8)]
            wave = wave_ref[f]
            turned = []
            for member, rows in enumerate(spans):
                weight_real, weight_imag = phase[member]
                g = along[member]
                wave_distance = wave * distance[member]
                dipole_real = g[0] * channel[2] + g[1] * channel[4] + g[2] * channel[6]
                dipole_imag = g[0] * channel[3] + g[1] * channel[5] + g[2] * channel[7]
                amp_real = channel[0] + dipole_real - wave_distance * dipole_imag
                amp_imag = channel[1] + dipole_imag + wave_distance * dipole_real
                acc_ref[f, 0, rows, :] += weight_real * amp_real + weight_imag * amp_imag
                acc_ref[f, 1, rows, :] += weight_real * amp_imag - weight_imag * amp_real
                turned.append(
                    (
                        weight_real * step_cos[member] - weight_imag * step_sin[member],
                        weight_imag * step_cos[member] + weight_real * step_sin[member],
                    )
                )
            return tuple(turned)

        start = tuple((geo_ref[0, rows, :], geo_ref[1, rows, :]) for rows in spans)
        lax.fori_loop(0, freqs, freq_body, start, unroll=freq_unroll)
        return carry

    lax.fori_loop(0, blocks // block_group, block_body, 0)

    @pl.when(pl.program_id(0) == pl.num_programs(0) - 1)
    def _():
        flat = acc_ref[...].reshape(freqs * 2 * observers, lanes)
        out_ref[...] = lax.dot_general(
            jnp.ones((8, lanes), jnp.float32),
            flat,
            (((1,), (1,)), ((), ())),
            precision=lax.Precision.HIGH,
            preferred_element_type=jnp.float32,
        )


def far_field(portion, panel_position, observer_position, wave_numbers):
    panel_total, columns = portion.shape
    freqs = columns // 8
    observers = observer_position.shape[1]
    offsets = observer_position[:, :, None] - panel_position[:, None, :]
    distance = jnp.sqrt(offsets[0] * offsets[0] + offsets[1] * offsets[1] + offsets[2] * offsets[2])
    inverse = 1.0 / distance
    first_phase = wave_numbers[0] * distance
    step_phase = wave_step * distance
    geometry = jnp.stack(
        [
            jnp.cos(first_phase) * inverse,
            jnp.sin(first_phase) * inverse,
            jnp.cos(step_phase),
            jnp.sin(step_phase),
            offsets[0] * inverse * inverse,
            offsets[1] * inverse * inverse,
            offsets[2] * inverse * inverse,
            distance,
        ]
    )
    summed = pl.pallas_call(
        functools.partial(field_kernel, math.gcd(observers // 8, 4), 8),
        grid=(panel_total // 128,),
        in_specs=[
            pl.BlockSpec(memory_space=pltpu.SMEM),
            pl.BlockSpec((8, observers, 128), lambda chunk: (0, 0, chunk)),
            pl.BlockSpec((128, columns), lambda chunk: (chunk, 0)),
        ],
        out_specs=pl.BlockSpec((8, freqs * 2 * observers), lambda chunk: (0, 0)),
        out_shape=jax.ShapeDtypeStruct((8, freqs * 2 * observers), jnp.float32),
        scratch_shapes=[
            pltpu.VMEM((freqs, 2, observers, 128), jnp.float32),
            pltpu.VMEM((columns, 128), jnp.float32),
        ],
        compiler_params=pltpu.CompilerParams(dimension_semantics=("arbitrary",)),
    )(wave_numbers, geometry, portion)
    return summed[0].reshape(freqs, 2, observers)


def partner_pairs(groups, bit):
    return [(k, k ^ bit) for k in range(groups)]


def quad_pairs(groups, shift):
    low = groups // 4
    return [(k, ((k // low + shift) % 4) * low + k % low) for k in range(groups)]


def halving_sum(blocks, bits):
    groups = blocks.shape[0]
    place = lax.axis_index("obs")
    current = blocks
    for bit in bits:
        split = current.reshape((current.shape[0] // 2, 2) + current.shape[1:])
        mine = (place // bit) % 2
        keep = lax.dynamic_index_in_dim(split, mine, 1, keepdims=False)
        send = lax.dynamic_index_in_dim(split, 1 - mine, 1, keepdims=False)
        current = keep + lax.ppermute(send, "obs", partner_pairs(groups, bit))
    quarter = place // (groups // 4)
    total = lax.dynamic_index_in_dim(current, quarter, 0, keepdims=False)
    for shift in (1, 2, 3):
        piece = lax.dynamic_index_in_dim(current, (quarter + shift) % 4, 0, keepdims=False)
        total = total + lax.ppermute(piece, "obs", quad_pairs(groups, shift))
    return total


def doubling_gather(own, bits, groups):
    place = lax.axis_index("obs")
    quarter = place // (groups // 4)
    arrived = jnp.stack(
        [own] + [lax.ppermute(own, "obs", quad_pairs(groups, shift)) for shift in (1, 2, 3)]
    )
    gathered = jnp.stack(
        [lax.dynamic_index_in_dim(arrived, (quarter - k) % 4, 0, keepdims=False) for k in range(4)]
    )
    for bit in reversed(bits):
        mine = (place // bit) % 2
        other = lax.ppermute(gathered, "obs", partner_pairs(groups, bit))
        low = jnp.where(mine == 0, gathered, other)
        high = jnp.where(mine == 0, other, gathered)
        gathered = jnp.stack([low, high], axis=1).reshape((-1,) + gathered.shape[1:])
    return gathered


def shards(cell_spectra, cell_weight, cell_owner, cell_local, panel_position, observer_position):
    cell_rows, columns = cell_spectra.shape
    freqs_dev = columns // 8
    groups = lax.axis_size("obs")
    panel_total = panel_position.shape[1]
    panels_dev = panel_total // groups
    weighted = (cell_weight[:, None] * cell_spectra.astype(jnp.float32)).astype(jnp.bfloat16)
    panel_number = jnp.arange(panel_total, dtype=jnp.int32)[:, None]
    selector = (
        (panel_number // panels_dev == cell_owner[:, 0][None, :])
        & (panel_number % panels_dev == cell_local[None, :])
    ).astype(jnp.bfloat16)
    local_source = jnp.dot(selector, weighted, preferred_element_type=jnp.float32)
    group_first = lax.axis_index("freq") * freqs_dev
    wave_numbers = wave_step * (
        (group_first + jnp.arange(freqs_dev, dtype=jnp.int32)).astype(jnp.float32) + 1.0
    )
    blocks = local_source.reshape(groups, panels_dev, columns)
    if groups & (groups - 1) == 0 and groups >= 4:
        bits = [1 << k for k in range(groups.bit_length() - 3)]
        own_source = halving_sum(blocks, bits)
        portion = doubling_gather(own_source, bits, groups).reshape(panel_total, columns)
    else:
        own_source = jnp.sum(lax.all_to_all(blocks, "obs", 0, 0, tiled=True), axis=0)
        portion = lax.all_to_all(
            jnp.broadcast_to(own_source[None], blocks.shape), "obs", 0, 0, tiled=True
        ).reshape(panel_total, columns)
    summed = far_field(portion, panel_position, observer_position, wave_numbers)
    pressure = summed * (reference_radius / math.sqrt(panel_total))
    energy = jnp.sum(pressure[:, 0] * pressure[:, 0] + pressure[:, 1] * pressure[:, 1], axis=0)
    if lax.axis_size("freq") == 2:
        band_total = energy + lax.ppermute(energy, "freq", [(0, 1), (1, 0)])
    else:
        band_total = lax.psum(energy, "freq")
    level = jnp.log(band_total / (freqs_dev * lax.axis_size("freq")) + 1e-06)
    return (pressure, level)


def solution(mesh):
    in_specs = (P("obs", "freq"), P("obs"), P("obs", None), P("obs"), P(), P(None, "obs"))
    out_specs = (P("freq", None, "obs"), P("obs"))
    return jax.shard_map(shards, mesh=mesh, in_specs=in_specs, out_specs=out_specs, check_vma=False)
```

```python
import functools
import math

import jax
import jax.numpy as jnp
from jax import lax
from jax.experimental import pallas as pl
from jax.experimental.pallas import tpu as pltpu
from jax.sharding import PartitionSpec as P

wave_step = 0.1
reference_radius = 10.0


def field_kernel(block_group, freq_unroll, wave_ref, geo_ref, src_ref, out_ref, acc_ref, chan_ref):
    freqs, _, observers, lanes = acc_ref.shape
    blocks = observers // 8

    @pl.when(pl.program_id(0) == 0)
    def _():
        acc_ref[...] = jnp.zeros(acc_ref.shape, acc_ref.dtype)

    chan_ref[...] = jnp.transpose(src_ref[...])


    def block_body(group, carry):
        spans = [
            pl.ds(pl.multiple_of((group * block_group + member) * 8, 8), 8)
            for member in range(block_group)
        ]
        step_cos = [geo_ref[2, rows, :] for rows in spans]
        step_sin = [geo_ref[3, rows, :] for rows in spans]
        along = [[geo_ref[4 + j, rows, :] for j in range(3)] for rows in spans]
        distance = [geo_ref[7, rows, :] for rows in spans]

        def freq_body(f, phase):
            base = f * 8
            channel = [chan_ref[pl.ds(base + c, 8, stride=0), :] for c in range(8)]
            wave = wave_ref[f]
            turned = []
            for member, rows in enumerate(spans):
                weight_real, weight_imag = phase[member]
                g = along[member]
                wave_distance = wave * distance[member]
                dipole_real = g[0] * channel[2] + g[1] * channel[4] + g[2] * channel[6]
                dipole_imag = g[0] * channel[3] + g[1] * channel[5] + g[2] * channel[7]
                amp_real = channel[0] + dipole_real - wave_distance * dipole_imag
                amp_imag = channel[1] + dipole_imag + wave_distance * dipole_real
                acc_ref[f, 0, rows, :] += weight_real * amp_real + weight_imag * amp_imag
                acc_ref[f, 1, rows, :] += weight_real * amp_imag - weight_imag * amp_real
                turned.append(
                    (
                        weight_real * step_cos[member] - weight_imag * step_sin[member],
                        weight_imag * step_cos[member] + weight_real * step_sin[member],
                    )
                )
            return tuple(turned)

        start = tuple((geo_ref[0, rows, :], geo_ref[1, rows, :]) for rows in spans)
        lax.fori_loop(0, freqs, freq_body, start, unroll=freq_unroll)
        return carry

    lax.fori_loop(0, blocks // block_group, block_body, 0)

    @pl.when(pl.program_id(0) == pl.num_programs(0) - 1)
    def _():
        flat = acc_ref[...].reshape(freqs * 2 * observers, lanes)
        out_ref[...] = lax.dot_general(
            jnp.ones((8, lanes), jnp.float32),
            flat,
            (((1,), (1,)), ((), ())),
            precision=lax.Precision.HIGH,
            preferred_element_type=jnp.float32,
        )


def far_field(portion, panel_position, observer_position, wave_numbers):
    panel_total, columns = portion.shape
    freqs = columns // 8
    observers = observer_position.shape[1]
    offsets = observer_position[:, :, None] - panel_position[:, None, :]
    distance = jnp.sqrt(offsets[0] * offsets[0] + offsets[1] * offsets[1] + offsets[2] * offsets[2])
    inverse = 1.0 / distance
    first_phase = wave_numbers[0] * distance
    step_phase = wave_step * distance
    geometry = jnp.stack(
        [
            jnp.cos(first_phase) * inverse,
            jnp.sin(first_phase) * inverse,
            jnp.cos(step_phase),
            jnp.sin(step_phase),
            offsets[0] * inverse * inverse,
            offsets[1] * inverse * inverse,
            offsets[2] * inverse * inverse,
            distance,
        ]
    )
    summed = pl.pallas_call(
        functools.partial(field_kernel, math.gcd(observers // 8, 4), 16),
        grid=(panel_total // 128,),
        in_specs=[
            pl.BlockSpec(memory_space=pltpu.SMEM),
            pl.BlockSpec((8, observers, 128), lambda chunk: (0, 0, chunk)),
            pl.BlockSpec((128, columns), lambda chunk: (chunk, 0)),
        ],
        out_specs=pl.BlockSpec((8, freqs * 2 * observers), lambda chunk: (0, 0)),
        out_shape=jax.ShapeDtypeStruct((8, freqs * 2 * observers), jnp.float32),
        scratch_shapes=[
            pltpu.VMEM((freqs, 2, observers, 128), jnp.float32),
            pltpu.VMEM((columns, 128), jnp.float32),
        ],
        compiler_params=pltpu.CompilerParams(dimension_semantics=("arbitrary",)),
    )(wave_numbers, geometry, portion)
    return summed[0].reshape(freqs, 2, observers)


def partner_pairs(groups, bit):
    return [(k, k ^ bit) for k in range(groups)]


def quad_pairs(groups, shift):
    low = groups // 4
    return [(k, ((k // low + shift) % 4) * low + k % low) for k in range(groups)]


def halving_sum(blocks, bits):
    groups = blocks.shape[0]
    place = lax.axis_index("obs")
    current = blocks
    for bit in bits:
        split = current.reshape((current.shape[0] // 2, 2) + current.shape[1:])
        mine = (place // bit) % 2
        keep = lax.dynamic_index_in_dim(split, mine, 1, keepdims=False)
        send = lax.dynamic_index_in_dim(split, 1 - mine, 1, keepdims=False)
        current = keep + lax.ppermute(send, "obs", partner_pairs(groups, bit))
    quarter = place // (groups // 4)
    total = lax.dynamic_index_in_dim(current, quarter, 0, keepdims=False)
    for shift in (1, 2, 3):
        piece = lax.dynamic_index_in_dim(current, (quarter + shift) % 4, 0, keepdims=False)
        total = total + lax.ppermute(piece, "obs", quad_pairs(groups, shift))
    return total


def doubling_gather(own, bits, groups):
    place = lax.axis_index("obs")
    quarter = place // (groups // 4)
    arrived = jnp.stack(
        [own] + [lax.ppermute(own, "obs", quad_pairs(groups, shift)) for shift in (1, 2, 3)]
    )
    gathered = jnp.stack(
        [lax.dynamic_index_in_dim(arrived, (quarter - k) % 4, 0, keepdims=False) for k in range(4)]
    )
    for bit in reversed(bits):
        mine = (place // bit) % 2
        other = lax.ppermute(gathered, "obs", partner_pairs(groups, bit))
        low = jnp.where(mine == 0, gathered, other)
        high = jnp.where(mine == 0, other, gathered)
        gathered = jnp.stack([low, high], axis=1).reshape((-1,) + gathered.shape[1:])
    return gathered


def shards(cell_spectra, cell_weight, cell_owner, cell_local, panel_position, observer_position):
    cell_rows, columns = cell_spectra.shape
    freqs_dev = columns // 8
    groups = lax.axis_size("obs")
    panel_total = panel_position.shape[1]
    panels_dev = panel_total // groups
    weighted = (cell_weight[:, None] * cell_spectra.astype(jnp.float32)).astype(jnp.bfloat16)
    panel_number = jnp.arange(panel_total, dtype=jnp.int32)[:, None]
    selector = (
        (panel_number // panels_dev == cell_owner[:, 0][None, :])
        & (panel_number % panels_dev == cell_local[None, :])
    ).astype(jnp.bfloat16)
    local_source = jnp.dot(selector, weighted, preferred_element_type=jnp.float32)
    group_first = lax.axis_index("freq") * freqs_dev
    wave_numbers = wave_step * (
        (group_first + jnp.arange(freqs_dev, dtype=jnp.int32)).astype(jnp.float32) + 1.0
    )
    blocks = local_source.reshape(groups, panels_dev, columns)
    if groups & (groups - 1) == 0 and groups >= 4:
        bits = [1 << k for k in range(groups.bit_length() - 3)]
        own_source = halving_sum(blocks, bits)
        portion = doubling_gather(own_source, bits, groups).reshape(panel_total, columns)
    else:
        own_source = jnp.sum(lax.all_to_all(blocks, "obs", 0, 0, tiled=True), axis=0)
        portion = lax.all_to_all(
            jnp.broadcast_to(own_source[None], blocks.shape), "obs", 0, 0, tiled=True
        ).reshape(panel_total, columns)
    summed = far_field(portion, panel_position, observer_position, wave_numbers)
    pressure = summed * (reference_radius / math.sqrt(panel_total))
    energy = jnp.sum(pressure[:, 0] * pressure[:, 0] + pressure[:, 1] * pressure[:, 1], axis=0)
    if lax.axis_size("freq") == 2:
        band_total = energy + lax.ppermute(energy, "freq", [(0, 1), (1, 0)])
    else:
        band_total = lax.psum(energy, "freq")
    level = jnp.log(band_total / (freqs_dev * lax.axis_size("freq")) + 1e-06)
    return (pressure, level)


def solution(mesh):
    in_specs = (P("obs", "freq"), P("obs"), P("obs", None), P("obs"), P(), P(None, "obs"))
    out_specs = (P("freq", None, "obs"), P("obs"))
    return jax.shard_map(shards, mesh=mesh, in_specs=in_specs, out_specs=out_specs, check_vma=False)
```

```python
import functools
import math

import jax
import jax.numpy as jnp
from jax import lax
from jax.experimental import pallas as pl
from jax.experimental.pallas import tpu as pltpu
from jax.sharding import PartitionSpec as P

wave_step = 0.1
reference_radius = 10.0


def field_kernel(block_group, freq_unroll, wave_ref, geo_ref, src_ref, out_ref, acc_ref, chan_ref):
    freqs, _, observers, lanes = acc_ref.shape
    blocks = observers // 8

    @pl.when(pl.program_id(0) == 0)
    def _():
        acc_ref[...] = jnp.zeros(acc_ref.shape, acc_ref.dtype)

    chan_ref[...] = jnp.transpose(src_ref[...])


    def block_body(group, carry):
        spans = [
            pl.ds(pl.multiple_of((group * block_group + member) * 8, 8), 8)
            for member in range(block_group)
        ]
        step_cos = [geo_ref[2, rows, :] for rows in spans]
        step_sin = [geo_ref[3, rows, :] for rows in spans]
        along = [[geo_ref[4 + j, rows, :] for j in range(3)] for rows in spans]
        distance = [geo_ref[7, rows, :] for rows in spans]

        def freq_body(f, phase):
            base = f * 8
            channel = [chan_ref[pl.ds(base + c, 8, stride=0), :] for c in range(8)]
            wave = wave_ref[f]
            turned = []
            for member, rows in enumerate(spans):
                weight_real, weight_imag = phase[member]
                g = along[member]
                wave_distance = wave * distance[member]
                dipole_real = g[0] * channel[2] + g[1] * channel[4] + g[2] * channel[6]
                dipole_imag = g[0] * channel[3] + g[1] * channel[5] + g[2] * channel[7]
                amp_real = channel[0] + dipole_real - wave_distance * dipole_imag
                amp_imag = channel[1] + dipole_imag + wave_distance * dipole_real
                acc_ref[f, 0, rows, :] += weight_real * amp_real + weight_imag * amp_imag
                acc_ref[f, 1, rows, :] += weight_real * amp_imag - weight_imag * amp_real
                turned.append(
                    (
                        weight_real * step_cos[member] - weight_imag * step_sin[member],
                        weight_imag * step_cos[member] + weight_real * step_sin[member],
                    )
                )
            return tuple(turned)

        start = tuple((geo_ref[0, rows, :], geo_ref[1, rows, :]) for rows in spans)
        lax.fori_loop(0, freqs, freq_body, start, unroll=freq_unroll)
        return carry

    lax.fori_loop(0, blocks // block_group, block_body, 0)

    @pl.when(pl.program_id(0) == pl.num_programs(0) - 1)
    def _():
        flat = acc_ref[...].reshape(freqs * 2 * observers, lanes)
        out_ref[...] = lax.dot_general(
            jnp.ones((8, lanes), jnp.float32),
            flat,
            (((1,), (1,)), ((), ())),
            precision=lax.Precision.HIGH,
            preferred_element_type=jnp.float32,
        )


def far_field(portion, panel_position, observer_position, wave_numbers):
    panel_total, columns = portion.shape
    freqs = columns // 8
    observers = observer_position.shape[1]
    offsets = observer_position[:, :, None] - panel_position[:, None, :]
    distance = jnp.sqrt(offsets[0] * offsets[0] + offsets[1] * offsets[1] + offsets[2] * offsets[2])
    inverse = 1.0 / distance
    first_phase = wave_numbers[0] * distance
    step_phase = wave_step * distance
    geometry = jnp.stack(
        [
            jnp.cos(first_phase) * inverse,
            jnp.sin(first_phase) * inverse,
            jnp.cos(step_phase),
            jnp.sin(step_phase),
            offsets[0] * inverse * inverse,
            offsets[1] * inverse * inverse,
            offsets[2] * inverse * inverse,
            distance,
        ]
    )
    summed = pl.pallas_call(
        functools.partial(field_kernel, math.gcd(observers // 8, 4), 32),
        grid=(panel_total // 128,),
        in_specs=[
            pl.BlockSpec(memory_space=pltpu.SMEM),
            pl.BlockSpec((8, observers, 128), lambda chunk: (0, 0, chunk)),
            pl.BlockSpec((128, columns), lambda chunk: (chunk, 0)),
        ],
        out_specs=pl.BlockSpec((8, freqs * 2 * observers), lambda chunk: (0, 0)),
        out_shape=jax.ShapeDtypeStruct((8, freqs * 2 * observers), jnp.float32),
        scratch_shapes=[
            pltpu.VMEM((freqs, 2, observers, 128), jnp.float32),
            pltpu.VMEM((columns, 128), jnp.float32),
        ],
        compiler_params=pltpu.CompilerParams(dimension_semantics=("arbitrary",)),
    )(wave_numbers, geometry, portion)
    return summed[0].reshape(freqs, 2, observers)


def partner_pairs(groups, bit):
    return [(k, k ^ bit) for k in range(groups)]


def quad_pairs(groups, shift):
    low = groups // 4
    return [(k, ((k // low + shift) % 4) * low + k % low) for k in range(groups)]


def halving_sum(blocks, bits):
    groups = blocks.shape[0]
    place = lax.axis_index("obs")
    current = blocks
    for bit in bits:
        split = current.reshape((current.shape[0] // 2, 2) + current.shape[1:])
        mine = (place // bit) % 2
        keep = lax.dynamic_index_in_dim(split, mine, 1, keepdims=False)
        send = lax.dynamic_index_in_dim(split, 1 - mine, 1, keepdims=False)
        current = keep + lax.ppermute(send, "obs", partner_pairs(groups, bit))
    quarter = place // (groups // 4)
    total = lax.dynamic_index_in_dim(current, quarter, 0, keepdims=False)
    for shift in (1, 2, 3):
        piece = lax.dynamic_index_in_dim(current, (quarter + shift) % 4, 0, keepdims=False)
        total = total + lax.ppermute(piece, "obs", quad_pairs(groups, shift))
    return total


def doubling_gather(own, bits, groups):
    place = lax.axis_index("obs")
    quarter = place // (groups // 4)
    arrived = jnp.stack(
        [own] + [lax.ppermute(own, "obs", quad_pairs(groups, shift)) for shift in (1, 2, 3)]
    )
    gathered = jnp.stack(
        [lax.dynamic_index_in_dim(arrived, (quarter - k) % 4, 0, keepdims=False) for k in range(4)]
    )
    for bit in reversed(bits):
        mine = (place // bit) % 2
        other = lax.ppermute(gathered, "obs", partner_pairs(groups, bit))
        low = jnp.where(mine == 0, gathered, other)
        high = jnp.where(mine == 0, other, gathered)
        gathered = jnp.stack([low, high], axis=1).reshape((-1,) + gathered.shape[1:])
    return gathered


def shards(cell_spectra, cell_weight, cell_owner, cell_local, panel_position, observer_position):
    cell_rows, columns = cell_spectra.shape
    freqs_dev = columns // 8
    groups = lax.axis_size("obs")
    panel_total = panel_position.shape[1]
    panels_dev = panel_total // groups
    weighted = (cell_weight[:, None] * cell_spectra.astype(jnp.float32)).astype(jnp.bfloat16)
    panel_number = jnp.arange(panel_total, dtype=jnp.int32)[:, None]
    selector = (
        (panel_number // panels_dev == cell_owner[:, 0][None, :])
        & (panel_number % panels_dev == cell_local[None, :])
    ).astype(jnp.bfloat16)
    local_source = jnp.dot(selector, weighted, preferred_element_type=jnp.float32)
    group_first = lax.axis_index("freq") * freqs_dev
    wave_numbers = wave_step * (
        (group_first + jnp.arange(freqs_dev, dtype=jnp.int32)).astype(jnp.float32) + 1.0
    )
    blocks = local_source.reshape(groups, panels_dev, columns)
    if groups & (groups - 1) == 0 and groups >= 4:
        bits = [1 << k for k in range(groups.bit_length() - 3)]
        own_source = halving_sum(blocks, bits)
        portion = doubling_gather(own_source, bits, groups).reshape(panel_total, columns)
    else:
        own_source = jnp.sum(lax.all_to_all(blocks, "obs", 0, 0, tiled=True), axis=0)
        portion = lax.all_to_all(
            jnp.broadcast_to(own_source[None], blocks.shape), "obs", 0, 0, tiled=True
        ).reshape(panel_total, columns)
    summed = far_field(portion, panel_position, observer_position, wave_numbers)
    pressure = summed * (reference_radius / math.sqrt(panel_total))
    energy = jnp.sum(pressure[:, 0] * pressure[:, 0] + pressure[:, 1] * pressure[:, 1], axis=0)
    if lax.axis_size("freq") == 2:
        band_total = energy + lax.ppermute(energy, "freq", [(0, 1), (1, 0)])
    else:
        band_total = lax.psum(energy, "freq")
    level = jnp.log(band_total / (freqs_dev * lax.axis_size("freq")) + 1e-06)
    return (pressure, level)


def solution(mesh):
    in_specs = (P("obs", "freq"), P("obs"), P("obs", None), P("obs"), P(), P(None, "obs"))
    out_specs = (P("freq", None, "obs"), P("obs"))
    return jax.shard_map(shards, mesh=mesh, in_specs=in_specs, out_specs=out_specs, check_vma=False)
```
